32 devices in a mesh: dp: 8 (over y, x, core), expert: 4 (over z).
Axes of the slice: x: 2, y: 2, z: 4, core: 2. Of those that a mesh axis runs over, the one named last changes fastest.
Arguments:
- hidden: bfloat16 [2, 512, 2880], P(None, ('dp', 'expert')), may hold values from -1.5 to 1.5
- norm_gain: float32 [2880], replicated, may hold values from 0.1 to 1.9
- router: bfloat16 [2880, 64], replicated, may hold values from -0.078125 to 0.078125
- routes: int32 [2, 512, 4], P(None, ('dp', 'expert')), may hold values from 0 to 63, all different within a row; in each aligned block of 16 rows (0 to 15, 16 to 31, ..., all dimensions but the last counted through in order) at most 2 rows name the same one
- w_gate: bfloat16 [64, 2880, 2048], P('expert', None, 'dp'), may hold values from -0.109375 to 0.109375
- w_up: bfloat16 [64, 2880, 2048], P('expert', None, 'dp'), may hold values from -0.109375 to 0.109375
- w_down: bfloat16 [64, 2048, 2880], P('expert', 'dp'), may hold values from -0.125 to 0.125
- queries: bfloat16 [2, 512, 4096], P(None, ('dp', 'expert')), may hold values from -5.5 to 5.5
- new_key: bfloat16 [2, 512, 512], P(None, ('dp', 'expert')), may hold values from -8 to 8
- new_value: bfloat16 [2, 512, 512], P(None, ('dp', 'expert')), may hold values from -6 to 6
- key_pages: bfloat16 [256, 4, 16, 512], P(('dp', 'expert')), may hold values from -6 to 6
- value_pages: bfloat16 [256, 4, 16, 512], P(('dp', 'expert')), may hold values from -6 to 6
- page_counts: int32 [32, 16], P(('dp', 'expert')), may hold values from 1 to 10, 32 in all within a row
- page_order: int32 [32, 32], P(('dp', 'expert')), may hold values from 0 to 31, each once within a row
Outputs:
- context: bfloat16 [2, 512, 4096], P(None, ('dp', 'expert'))
- layer_out: bfloat16 [2, 512, 2880], P(None, ('dp', 'expert'))
The draws below stay inside these ranges and needn't reach their ends.
Inputs may be any that keep to these rules, and one draw needn't show every extreme that they name: `routes`: in each step, the 16 rows of one aligned block name each expert at most 2 times, and some block names some expert exactly 2 times. `page_counts`: each block's counts sum to 32, and the largest count of a block is exactly 10. Each row of page_order is a permutation of 0 to 31.
All inputs are finite; a program needn't handle non-finite values.
Results may differ from the reference program's by a relative error of at most 0.0095.
Values may be sent and summed in bfloat16 or wider, within the bound.
No kernel may reach another device: no remote copies, remote signals or barrier semaphores. Data moves between devices by JAX's collectives and lax.ppermute only.
A program may use at most 192 MiB of HBM per device.

```python
import math
import jax
import jax.numpy as jnp
import numpy as np
from jax import lax

D = 2880
HEADS = 64
KV_HEADS = 8
HEAD_DIM = 64
EXPERTS = 64
TOPK = 4
FF = 2048
MOST = 2
STEPS = 2
BLOCK = 16
ROWS_DEV = 16
PAGE_HOST = 4
ROWS = 512
PAGES_DEV = 32
MAXP = 10
N_DP = 8
N_EXPERT = 4


def draw_queries(key, part):
    base_key = jax.random.fold_in(key, 11)
    group_size = HEADS // KV_HEADS
    shape = (STEPS, ROWS, KV_HEADS, group_size, HEAD_DIM)
    values = jax.random.truncated_normal(base_key, -4.0, 4.0, shape, jnp.float32)
    return values.reshape(STEPS, ROWS, HEADS * HEAD_DIM).astype(jnp.bfloat16)


def draw_key_pages(key, part):
    base_key = jax.random.fold_in(key, 19)
    shape = (N_DP * N_EXPERT * N_DP, PAGE_HOST, BLOCK, KV_HEADS, HEAD_DIM)
    values = jax.random.truncated_normal(base_key, -4.0, 4.0, shape, jnp.float32)
    return values.reshape(N_DP * N_EXPERT * N_DP, PAGE_HOST, BLOCK, KV_HEADS * HEAD_DIM).astype(jnp.bfloat16)


def block_levels(rng, shape, cuts, low, high):
    def one(dim, parts):
        draws = jax.random.uniform(jax.random.fold_in(jax.random.fold_in(rng, 6), dim), (parts,), jnp.float32, low / len(cuts), high / len(cuts))
        return jnp.repeat(jnp.exp(draws), shape[dim] // parts).reshape((-1,) + (1,) * (len(shape) - dim - 1))

    level = one(*cuts[0])
    for cut in cuts[1:]:
        level = level * one(*cut)
    return level


def profile(count, total, reach, lean):
    weights = [(1 << 20) // math.isqrt(rank ** lean) + 1 for rank in range(2, count + 1)]
    spare, given = total - reach - (count - 1), [1] * (count - 1)
    while spare > 0:
        free = [i for i in range(count - 1) if given[i] < reach]
        whole, budget = sum([weights[i] for i in free]), spare
        for i in free:
            addition = min(reach - given[i], max(1, budget * weights[i] // whole), spare)
            given[i] = given[i] + addition
            spare = spare - addition
    return np.array([reach] + given)


def uneven(key, amount, total, reach, lean):
    if amount == 2:
        one = jax.random.randint(key, (), max(1, total - reach), min(reach, total - 1) + 1)
        return jnp.stack([one, total - one])
    tallies = jnp.asarray(profile(amount, total, reach, lean), jnp.int32)
    couples = (amount - 1) // 2
    donor, sink = tallies[1:1 + 2 * couples:2], tallies[2:2 + 2 * couples:2]
    slack = jnp.minimum(donor - 1, reach - sink)
    shifted = jax.random.randint(jax.random.fold_in(key, 1), (couples,), 0, 1 << 20) % (slack + 1)
    tallies = tallies.at[1:1 + 2 * couples:2].set(donor - shifted).at[2:2 + 2 * couples:2].set(sink + shifted)
    return tallies[jax.random.permutation(jax.random.fold_in(key, 2), amount)]


def shared_out(rng, own, number, rows, amount, top, limit, lean):
    ranking = jax.random.permutation(rng, amount)
    heavy_load, ordinary = portions_of(amount, rows * top, limit, lean, True), portions_of(amount, rows * top, limit, lean, False)
    places = jnp.arange(amount)

    def named(sizes, offset_by):
        used = int((sizes > 0).sum())
        fixed = max(1, used // 4)
        moved = fixed + (places - fixed + offset_by * (used - fixed)) % max(1, amount - fixed)
        return jnp.zeros((amount,), jnp.int32).at[ranking[jnp.where(places < fixed, places, moved)]].set(jnp.asarray(sizes, jnp.int32))

    sizes = jnp.where(number % 4 == 0, named(heavy_load, number // 4), named(ordinary, number - number // 4 - 1))
    mixed = jax.random.permutation(jax.random.fold_in(own, 3), amount)
    source_of, receiver = mixed[0:amount // 2 * 2:2], mixed[1:amount // 2 * 2:2]
    margin = jnp.minimum(sizes[source_of] - 1, limit - sizes[receiver]) // 2
    margin = jnp.where((source_of == ranking[0]) | (receiver == ranking[0]) | (sizes[receiver] == 0), 0, jnp.maximum(margin, 0))
    moved = jax.random.randint(jax.random.fold_in(own, 4), (amount // 2,), 0, 1 << 20) % (margin + 1)
    sizes = sizes.at[source_of].add(-moved).at[receiver].add(moved)
    labels = jnp.searchsorted(jnp.cumsum(sizes), jnp.arange(rows * top), side="right").astype(jnp.int32)
    table = labels.reshape(top, rows).T
    table = table[jax.random.permutation(jax.random.fold_in(own, 1), rows)]
    offset_by = jax.random.randint(jax.random.fold_in(own, 2), (rows, 1), 0, top)
    return jnp.take_along_axis(table, (jnp.arange(top)[None, :] + offset_by) % top, axis=1)


def portions_of(count, total, limit, slope, full):
    weights = [(1 << 20) // math.isqrt(standing ** slope) + 1 for standing in range(1, count + 1)]
    largest = limit if full else min(limit, max(-(-total // count), total * weights[0] // sum(weights)))
    least = 1 if total - largest >= count - 1 else 0
    given, spare = [largest] + [least] * (count - 1), total - largest - least * (count - 1)
    while spare > 0:
        movable = [i for i in range(1, count) if given[i] < largest] or [i for i in range(1, count) if given[i] < limit]
        pool, left = sum([weights[i] for i in movable]), spare
        for i in movable:
            extra = min(limit - given[i], max(1, left * weights[i] // pool), spare)
            given[i] = given[i] + extra
            spare = spare - extra
    return np.array(given)


def normal_values(stream_key, extent, deviation, bound, split=(), kind=jnp.bfloat16):
    values = jax.random.normal(stream_key, extent, jnp.float32) * deviation
    if len(split) > 0:
        values = block_levels(stream_key, extent, split, -0.22, 0.18) * values
    return jnp.clip(values, min=-bound, max=bound).astype(kind)


def setup_inputs(seed: int = 0) -> dict:
    key_list = jax.random.split(jax.random.key(seed), 15)
    hidden = normal_values(key_list[0], (STEPS, ROWS, D), 0.25, 1.5, ((1, 32),))
    norm_gain = jnp.clip(1.0 + 0.18 * jax.random.normal(key_list[1], (D,), jnp.float32), 0.1, 1.9)
    router = normal_values(key_list[2], (D, EXPERTS), (2 * D) ** -0.5, 0.078125)
    routes_keys = jax.random.split(jax.random.fold_in(key_list[3], 1), STEPS * ROWS // ROWS_DEV)
    routes_turns = jax.random.permutation(jax.random.fold_in(key_list[3], 3), STEPS * ROWS // ROWS_DEV)
    routes = jax.vmap(lambda own, number: shared_out(jax.random.fold_in(key_list[3], 2), own, number, ROWS_DEV, EXPERTS, TOPK, MOST, 2))(routes_keys, routes_turns).reshape((STEPS, ROWS, TOPK))
    w_gate = normal_values(key_list[4], (EXPERTS, D, FF), D ** -0.5, 0.109375, ((0, 4), (2, 8)))
    w_up = normal_values(key_list[5], (EXPERTS, D, FF), D ** -0.5, 0.109375, ((0, 4), (2, 8)))
    w_down = normal_values(key_list[6], (EXPERTS, FF, D), FF ** -0.5, 0.125, ((0, 4), (1, 8)))
    queries = draw_queries(jax.random.fold_in(key_list[14], 71), 0)
    new_key = normal_values(key_list[8], (STEPS, ROWS, KV_HEADS * HEAD_DIM), 2.0, 8.0, ((1, 32),))
    new_value = normal_values(key_list[9], (STEPS, ROWS, KV_HEADS * HEAD_DIM), 1.0, 6.0, ((1, 32),))
    key_pages = draw_key_pages(jax.random.fold_in(key_list[14], 71), 0)
    value_pages = normal_values(key_list[11], (N_DP * N_EXPERT * N_DP, PAGE_HOST, BLOCK, KV_HEADS * HEAD_DIM), 1.0, 6.0, ((0, 32),))
    page_counts = jax.vmap(lambda own: uneven(own, ROWS_DEV, PAGES_DEV, MAXP, 2))(jax.random.split(key_list[12], (N_DP * N_EXPERT))).reshape((N_DP * N_EXPERT, ROWS_DEV)).astype(jnp.int32)
    page_order = jax.vmap(lambda own: jax.random.permutation(own, PAGES_DEV))(jax.random.split(key_list[13], (N_DP * N_EXPERT))).reshape((N_DP * N_EXPERT, PAGES_DEV)).astype(jnp.int32)
    return dict(hidden=hidden, norm_gain=norm_gain, router=router, routes=routes, w_gate=w_gate, w_up=w_up, w_down=w_down, queries=queries, new_key=new_key, new_value=new_value, key_pages=key_pages, value_pages=value_pages, page_counts=page_counts, page_order=page_order)


def page_layout(counts, page_perm):
    starts = jnp.cumsum(counts) - counts
    offsets = jnp.arange(MAXP, dtype=jnp.int32)
    places = starts[:, None] + offsets[None, :]
    places = jnp.where(offsets[None, :] < counts[:, None], places, 0).astype(jnp.int32)
    return jnp.take(page_perm, places, axis=0)

def attend_block(operands):
    query_rows, fresh_keys, fresh_values, space_keys, space_values, counts, page_perm = operands
    group_size = HEADS // KV_HEADS
    row_count = counts.shape[0]
    cache_span = MAXP * BLOCK
    slot_ids = page_layout(counts, page_perm).reshape(-1)
    cache_keys = jnp.take(space_keys, slot_ids, axis=0).reshape(row_count, cache_span, KV_HEADS, HEAD_DIM).astype(jnp.float32)
    cache_values = jnp.take(space_values, slot_ids, axis=0).reshape(row_count, cache_span, KV_HEADS, HEAD_DIM).astype(jnp.float32)
    live_mask = jnp.arange(cache_span)[None, :] < (counts * BLOCK)[:, None]
    query_heads = query_rows.reshape(STEPS, row_count, KV_HEADS, group_size, HEAD_DIM).astype(jnp.float32)
    new_keys = fresh_keys.reshape(STEPS, row_count, KV_HEADS, HEAD_DIM).astype(jnp.float32)
    new_values = fresh_values.reshape(STEPS, row_count, KV_HEADS, HEAD_DIM).astype(jnp.float32)
    score_scale = HEAD_DIM ** (-0.5)
    old_scores = jnp.einsum('trkgh,rlkh->trkgl', query_heads, cache_keys) * score_scale
    old_scores = jnp.where(live_mask[None, :, None, None, :], old_scores, -jnp.inf)
    new_scores = jnp.einsum('trkgh,urkh->trkgu', query_heads, new_keys) * score_scale
    causal = jnp.arange(STEPS)[None, :] <= jnp.arange(STEPS)[:, None]
    new_scores = jnp.where(causal[:, None, None, None, :], new_scores, -jnp.inf)
    row_max = jnp.maximum(lax.optimization_barrier(jnp.max(old_scores, axis=-1)), lax.optimization_barrier(jnp.max(new_scores, axis=-1)))
    old_probs = jnp.exp(old_scores - row_max[..., None])
    new_probs = jnp.exp(new_scores - row_max[..., None])
    denominator = lax.optimization_barrier(jnp.sum(old_probs, axis=-1)) + lax.optimization_barrier(jnp.sum(new_probs, axis=-1))
    old_round = lax.optimization_barrier(old_probs.astype(jnp.bfloat16))
    new_round = lax.optimization_barrier(new_probs.astype(jnp.bfloat16))
    numerator = jnp.einsum('trkgl,rlkh->trkgh', old_round.astype(jnp.float32), cache_values)
    numerator = numerator + jnp.einsum('trkgu,urkh->trkgh', new_round.astype(jnp.float32), new_values)
    result = numerator / denominator[..., None]
    return result.reshape(STEPS, row_count, HEADS * HEAD_DIM).astype(jnp.bfloat16)

def expert_rows(operands):
    slot_rows, gate_w, up_w, down_w = operands
    gate_part = jnp.dot(slot_rows, gate_w, preferred_element_type=jnp.float32)
    up_part = jnp.dot(slot_rows, up_w, preferred_element_type=jnp.float32)
    hidden_act = ((up_part + 1.0) * gate_part * jax.nn.sigmoid(1.702 * gate_part)).astype(jnp.bfloat16)
    hidden_act = lax.optimization_barrier(hidden_act)
    act_blocks = hidden_act.reshape(slot_rows.shape[0], N_DP, FF // N_DP).astype(jnp.float32)
    down_blocks = down_w.reshape(N_DP, FF // N_DP, D).astype(jnp.float32)
    partials = jnp.einsum('snf,nfd->snd', act_blocks, down_blocks).astype(jnp.bfloat16)
    partials = lax.optimization_barrier(partials)
    return lax.optimization_barrier(jnp.sum(partials.astype(jnp.float32), axis=1))

def moe_layer(hidden_rows, norm_gain, router, expert_ids, w_gate, w_up, w_down):
    devices_all = N_DP * N_EXPERT
    residual = hidden_rows.astype(jnp.float32)
    scale_rows = lax.rsqrt(lax.optimization_barrier(jnp.mean(residual * residual, axis=1, keepdims=True)) + 1e-05)
    normed = (residual * scale_rows * norm_gain).astype(jnp.bfloat16)
    logit_rows = jnp.dot(normed, router, preferred_element_type=jnp.float32)
    chosen = jnp.take_along_axis(logit_rows, expert_ids, axis=1)
    spreads = chosen[:, None, :] - chosen[:, :, None]
    gate_vals = (1.0 / lax.optimization_barrier(jnp.sum(jnp.exp(spreads), axis=2))).astype(jnp.bfloat16)
    block_ids = expert_ids.reshape(devices_all, ROWS_DEV, TOPK)
    picked = (block_ids[..., None] == jnp.arange(EXPERTS, dtype=jnp.int32)).astype(jnp.int32)
    per_row = lax.optimization_barrier(jnp.sum(picked, axis=2))
    earlier = jnp.cumsum(per_row, axis=1) - per_row
    rank_vals = lax.optimization_barrier(jnp.sum(picked * earlier[:, :, None, :], axis=3))
    slot_ids = (jnp.arange(devices_all, dtype=jnp.int32)[:, None, None] * MOST + rank_vals).reshape(-1).astype(jnp.int32)
    flat_ids = expert_ids.reshape(-1).astype(jnp.int32)
    sources = jnp.broadcast_to(normed[:, None, :], (ROWS, TOPK, D)).reshape(-1, D)
    buffer = jnp.zeros((EXPERTS, devices_all * MOST, D), jnp.bfloat16).at[flat_ids, slot_ids].set(sources)
    results = lax.map(expert_rows, (buffer, w_gate, w_up, w_down))
    picked_out = results[flat_ids, slot_ids].reshape(ROWS, TOPK, D)
    branch_out = lax.optimization_barrier(jnp.sum(gate_vals.astype(jnp.float32)[:, :, None] * picked_out, axis=1))
    return (residual + branch_out).astype(jnp.bfloat16)

def reference(hidden, norm_gain, router, routes, w_gate, w_up, w_down, queries, new_key, new_value, key_pages, value_pages, page_counts, page_order):
    devices_all = N_DP * N_EXPERT
    kv_width = KV_HEADS * HEAD_DIM

    def regroup(pages):
        grid = pages.reshape(N_DP, N_EXPERT, N_DP, PAGE_HOST, BLOCK, kv_width)
        return jnp.transpose(grid, (2, 1, 0, 3, 4, 5)).reshape(devices_all, N_DP * PAGE_HOST, BLOCK, kv_width)

    def by_block(array):
        return jnp.moveaxis(array.reshape(STEPS, devices_all, ROWS_DEV, array.shape[-1]), 1, 0)
    contexts = lax.map(attend_block, (by_block(queries), by_block(new_key), by_block(new_value), regroup(key_pages), regroup(value_pages), page_counts, page_order))
    context = jnp.moveaxis(contexts, 0, 1).reshape(STEPS, ROWS, HEADS * HEAD_DIM)
    layers = []
    for step_index in range(STEPS):
        layers.append(moe_layer(hidden[step_index], norm_gain, router, routes[step_index], w_gate, w_up, w_down))
    return (context, jnp.stack(layers))
```

```python
import jax
import jax.numpy as jnp
from jax import lax
from jax.sharding import PartitionSpec as P

HEADS = 64
KV_HEADS = 8
HEAD_DIM = 64
EXPERTS = 64
MOST = 2
STEPS = 2
BLOCK = 16


def page_layout(counts, page_perm, most_pages):
    starts = jnp.cumsum(counts) - counts
    offsets = jnp.arange(most_pages, dtype=jnp.int32)
    places = starts[:, None] + offsets[None, :]
    places = jnp.where(offsets[None, :] < counts[:, None], places, 0)
    return jnp.take(page_perm, places, axis=0)


def attention(query_rows, fresh_keys, fresh_values, space_keys, space_values, counts, page_perm):
    group_size = HEADS // KV_HEADS
    most_pages = page_perm.shape[0] // 3
    row_count = counts.shape[0]
    cache_span = most_pages * BLOCK
    slot_ids = page_layout(counts, page_perm, most_pages).reshape(-1)
    cache_keys = jnp.take(space_keys, slot_ids, axis=0).reshape(
        row_count, cache_span, KV_HEADS, HEAD_DIM
    )
    cache_values = jnp.take(space_values, slot_ids, axis=0).reshape(
        row_count, cache_span, KV_HEADS, HEAD_DIM
    )
    live_mask = jnp.arange(cache_span)[None, :] < (counts * BLOCK)[:, None]
    query_heads = query_rows.reshape(STEPS, row_count, KV_HEADS, group_size, HEAD_DIM)
    new_keys = fresh_keys.reshape(STEPS, row_count, KV_HEADS, HEAD_DIM)
    new_values = fresh_values.reshape(STEPS, row_count, KV_HEADS, HEAD_DIM)
    score_scale = HEAD_DIM ** (-0.5)
    old_scores = (
        jnp.einsum("trkgh,rlkh->trkgl", query_heads, cache_keys, preferred_element_type=jnp.float32)
        * score_scale
    )
    old_scores = jnp.where(live_mask[None, :, None, None, :], old_scores, -jnp.inf)
    new_scores = (
        jnp.einsum("trkgh,urkh->trkgu", query_heads, new_keys, preferred_element_type=jnp.float32)
        * score_scale
    )
    causal = jnp.arange(STEPS)[None, :] <= jnp.arange(STEPS)[:, None]
    new_scores = jnp.where(causal[:, None, None, None, :], new_scores, -jnp.inf)
    row_max = jnp.maximum(jnp.max(old_scores, axis=-1), jnp.max(new_scores, axis=-1))
    old_probs = jnp.exp(old_scores - row_max[..., None])
    new_probs = jnp.exp(new_scores - row_max[..., None])
    denominator = jnp.sum(old_probs, axis=-1) + jnp.sum(new_probs, axis=-1)
    numerator = jnp.einsum(
        "trkgl,rlkh->trkgh",
        old_probs.astype(jnp.bfloat16),
        cache_values,
        preferred_element_type=jnp.float32,
    )
    numerator = numerator + jnp.einsum(
        "trkgu,urkh->trkgh",
        new_probs.astype(jnp.bfloat16),
        new_values,
        preferred_element_type=jnp.float32,
    )
    result = numerator / denominator[..., None]
    return result.reshape(STEPS, row_count, HEADS * HEAD_DIM).astype(jnp.bfloat16)


MOST = 2


def moe_layer(hidden, norm_gain, router, routes, w_gate, w_up, w_down):
    steps, rows, model_width = hidden.shape
    topk = routes.shape[-1]
    n_dp = lax.axis_size("dp")
    n_ex = lax.axis_size("expert")
    local_experts = w_gate.shape[0]
    blocks = n_dp * n_ex
    residual = hidden.astype(jnp.float32)
    scale_rows = lax.rsqrt(jnp.mean(residual * residual, axis=-1, keepdims=True) + 1e-05)
    normed = (residual * scale_rows * norm_gain).astype(jnp.bfloat16)
    logit_rows = jnp.einsum("trd,de->tre", normed, router, preferred_element_type=jnp.float32)
    chosen = jnp.take_along_axis(logit_rows, routes, axis=-1)
    spreads = chosen[..., None, :] - chosen[..., :, None]
    gate_vals = (1.0 / jnp.sum(jnp.exp(spreads), axis=-1)).astype(jnp.bfloat16)
    lanes = -(-(model_width + 2 * topk) // 128) * 128
    filler = jnp.zeros((steps, rows, lanes - model_width - 2 * topk), jnp.bfloat16)
    payload = jnp.concatenate(
        [normed, gate_vals, routes.astype(jnp.bfloat16), filler], axis=-1
    )
    gathered = lax.all_gather(payload, ("dp", "expert"), axis=1, tiled=False)
    all_rows = gathered[..., :model_width]
    all_gates = gathered[..., model_width : model_width + topk]
    all_ids = gathered[..., model_width + topk : model_width + 2 * topk].astype(jnp.int32)
    first = lax.axis_index("expert") * local_experts
    numbers = first + jnp.arange(local_experts, dtype=jnp.int32)
    matches = all_ids[..., None] == numbers
    picked = jnp.any(matches, axis=-2).astype(jnp.int32)
    gate_of = jnp.sum(jnp.where(matches, all_gates[..., None].astype(jnp.float32), 0.0), axis=-2)
    earlier = jnp.cumsum(picked, axis=2) - picked
    ranks = jnp.arange(MOST, dtype=jnp.int32)
    sender = (picked[..., None] > 0) & (earlier[..., None] == ranks)
    slots = jnp.einsum(
        "tbrxm,tbrd->tbxmd",
        sender.astype(jnp.bfloat16),
        all_rows,
        preferred_element_type=jnp.float32,
    ).astype(jnp.bfloat16)
    gate_part = jnp.einsum("tbxmd,xdf->tbxmf", slots, w_gate, preferred_element_type=jnp.float32)
    up_part = jnp.einsum("tbxmd,xdf->tbxmf", slots, w_up, preferred_element_type=jnp.float32)
    hidden_act = ((up_part + 1.0) * gate_part * jax.nn.sigmoid(1.702 * gate_part)).astype(
        jnp.bfloat16
    )
    partial = jnp.einsum(
        "tbxmf,xfd->tbxmd", hidden_act, w_down, preferred_element_type=jnp.float32
    ).astype(jnp.bfloat16)
    weights = jnp.where(sender, gate_of[..., None], 0.0).astype(jnp.bfloat16)
    grid = (steps, n_dp, n_ex)
    if local_experts * MOST < rows:
        summed = lax.psum_scatter(
            partial.astype(jnp.float32).reshape(grid + partial.shape[2:]),
            "dp",
            scatter_dimension=1,
            tiled=True,
        )[:, 0]
        own = lax.axis_index("dp")
        own_weights = lax.dynamic_index_in_dim(weights.reshape(grid + weights.shape[2:]), own, 1, False)
        row_terms = jnp.einsum(
            "terxm,texmd->terd",
            own_weights.astype(jnp.float32),
            summed,
            precision=lax.Precision.HIGHEST,
            preferred_element_type=jnp.float32,
        )
    else:
        row_terms = jnp.einsum(
            "tbrxm,tbxmd->tbrd", weights, partial, preferred_element_type=jnp.float32
        )
        row_terms = lax.psum_scatter(
            row_terms.reshape(grid + row_terms.shape[2:]), "dp", scatter_dimension=1, tiled=True
        )[:, 0]
    branch_out = lax.psum_scatter(row_terms, "expert", scatter_dimension=1, tiled=True)
    return (residual + branch_out[:, 0]).astype(jnp.bfloat16)


def body(
    hidden,
    norm_gain,
    router,
    routes,
    w_gate,
    w_up,
    w_down,
    queries,
    new_key,
    new_value,
    key_pages,
    value_pages,
    page_counts,
    page_order,
):
    host_keys, host_values = (
        lax.all_to_all(key_pages, "dp", split_axis=0, concat_axis=0, tiled=True),
        lax.all_to_all(value_pages, "dp", split_axis=0, concat_axis=0, tiled=True),
    )
    kv_width = KV_HEADS * HEAD_DIM
    space_keys = host_keys.reshape(-1, BLOCK, kv_width)
    space_values = host_values.reshape(-1, BLOCK, kv_width)
    context = attention(
        queries, new_key, new_value, space_keys, space_values, page_counts[0], page_order[0]
    )
    layer_out = moe_layer(hidden, norm_gain, router, routes, w_gate, w_up, w_down)
    return (context, layer_out)


def solution(mesh):
    return jax.shard_map(
        body,
        mesh=mesh,
        in_specs=(
            P(None, ("dp", "expert"), None),
            P(),
            P(),
            P(None, ("dp", "expert"), None),
            P("expert", None, "dp"),
            P("expert", None, "dp"),
            P("expert", "dp", None),
            P(None, ("dp", "expert"), None),
            P(None, ("dp", "expert"), None),
            P(None, ("dp", "expert"), None),
            P(("dp", "expert"), None, None, None),
            P(("dp", "expert"), None, None, None),
            P(("dp", "expert"), None),
            P(("dp", "expert"), None),
        ),
        out_specs=(P(None, ("dp", "expert"), None), P(None, ("dp", "expert"), None)),
        check_vma=False,
    )
```

```python
import jax
import jax.numpy as jnp
from jax import lax
from jax.sharding import PartitionSpec as P

HEADS = 64
KV_HEADS = 8
HEAD_DIM = 64
EXPERTS = 64
MOST = 2
STEPS = 2
BLOCK = 16


def page_layout(counts, page_perm, most_pages):
    starts = jnp.cumsum(counts) - counts
    offsets = jnp.arange(most_pages, dtype=jnp.int32)
    places = starts[:, None] + offsets[None, :]
    places = jnp.where(offsets[None, :] < counts[:, None], places, 0)
    return jnp.take(page_perm, places, axis=0)


def attention(query_rows, fresh_keys, fresh_values, space_keys, space_values, counts, page_perm):
    group_size = HEADS // KV_HEADS
    most_pages = page_perm.shape[0] // 3
    row_count = counts.shape[0]
    cache_span = most_pages * BLOCK
    slot_ids = page_layout(counts, page_perm, most_pages).reshape(-1)
    cache_keys = jnp.take(space_keys, slot_ids, axis=0).reshape(
        row_count, cache_span, KV_HEADS, HEAD_DIM
    )
    cache_values = jnp.take(space_values, slot_ids, axis=0).reshape(
        row_count, cache_span, KV_HEADS, HEAD_DIM
    )
    live_mask = jnp.arange(cache_span)[None, :] < (counts * BLOCK)[:, None]
    query_heads = query_rows.reshape(STEPS, row_count, KV_HEADS, group_size, HEAD_DIM)
    new_keys = fresh_keys.reshape(STEPS, row_count, KV_HEADS, HEAD_DIM)
    new_values = fresh_values.reshape(STEPS, row_count, KV_HEADS, HEAD_DIM)
    score_scale = HEAD_DIM ** (-0.5)
    old_scores = (
        jnp.einsum("trkgh,rlkh->trkgl", query_heads, cache_keys, preferred_element_type=jnp.float32)
        * score_scale
    )
    old_scores = jnp.where(live_mask[None, :, None, None, :], old_scores, -jnp.inf)
    new_scores = (
        jnp.einsum("trkgh,urkh->trkgu", query_heads, new_keys, preferred_element_type=jnp.float32)
        * score_scale
    )
    causal = jnp.arange(STEPS)[None, :] <= jnp.arange(STEPS)[:, None]
    new_scores = jnp.where(causal[:, None, None, None, :], new_scores, -jnp.inf)
    row_max = jnp.maximum(jnp.max(old_scores, axis=-1), jnp.max(new_scores, axis=-1))
    old_probs = jnp.exp(old_scores - row_max[..., None])
    new_probs = jnp.exp(new_scores - row_max[..., None])
    denominator = jnp.sum(old_probs, axis=-1) + jnp.sum(new_probs, axis=-1)
    numerator = jnp.einsum(
        "trkgl,rlkh->trkgh",
        old_probs.astype(jnp.bfloat16),
        cache_values,
        preferred_element_type=jnp.float32,
    )
    numerator = numerator + jnp.einsum(
        "trkgu,urkh->trkgh",
        new_probs.astype(jnp.bfloat16),
        new_values,
        preferred_element_type=jnp.float32,
    )
    result = numerator / denominator[..., None]
    return result.reshape(STEPS, row_count, HEADS * HEAD_DIM).astype(jnp.bfloat16)


MOST = 2


def sibling(x):
    n_dp = lax.axis_size("dp")
    pairs = [(i, i ^ 1) for i in range(n_dp)]
    return lax.ppermute(x, "dp", perm=pairs)


def moe_layer(hidden, norm_gain, router, routes, w_gate, w_up, w_down):
    steps, rows, model_width = hidden.shape
    topk = routes.shape[-1]
    n_dp = lax.axis_size("dp")
    n_ex = lax.axis_size("expert")
    local_experts = w_gate.shape[0]
    core = lax.axis_index("dp") % 2
    same_core = [[i for i in range(n_dp) if i % 2 == c] for c in range(2)]
    residual = hidden.astype(jnp.float32)
    scale_rows = lax.rsqrt(jnp.mean(residual * residual, axis=-1, keepdims=True) + 1e-05)
    normed = (residual * scale_rows * norm_gain).astype(jnp.bfloat16)
    logit_rows = jnp.einsum("trd,de->tre", normed, router, preferred_element_type=jnp.float32)
    chosen = jnp.take_along_axis(logit_rows, routes, axis=-1)
    spreads = chosen[..., None, :] - chosen[..., :, None]
    gate_vals = (1.0 / jnp.sum(jnp.exp(spreads), axis=-1)).astype(jnp.bfloat16)
    lanes = -(-(model_width + 2 * topk) // 128) * 128
    filler = jnp.zeros((steps, rows, lanes - model_width - 2 * topk), jnp.bfloat16)
    payload = jnp.concatenate(
        [normed, gate_vals, routes.astype(jnp.bfloat16), filler], axis=-1
    )
    mine = lax.dynamic_index_in_dim(payload, core, 0, keepdims=False)
    theirs = sibling(lax.dynamic_index_in_dim(payload, 1 - core, 0, keepdims=False))
    pair = jnp.where(core == 0, jnp.stack([mine, theirs]), jnp.stack([theirs, mine]))
    pair = lax.all_gather(pair, "expert", axis=0, tiled=False)
    gathered_mine = lax.all_gather(pair, "dp", axis=0, tiled=False, axis_index_groups=same_core)
    gathered = jnp.stack([gathered_mine, sibling(gathered_mine)])
    all_rows = gathered[..., :model_width]
    all_gates = gathered[..., model_width : model_width + topk]
    all_ids = gathered[..., model_width + topk : model_width + 2 * topk].astype(jnp.int32)
    first = lax.axis_index("expert") * local_experts
    numbers = first + jnp.arange(local_experts, dtype=jnp.int32)
    matches = all_ids[..., None] == numbers
    picked = jnp.any(matches, axis=-2).astype(jnp.int32)
    gate_of = jnp.sum(jnp.where(matches, all_gates[..., None].astype(jnp.float32), 0.0), axis=-2)
    earlier = jnp.cumsum(picked, axis=4) - picked
    ranks = jnp.arange(MOST, dtype=jnp.int32)
    sender = (picked[..., None] > 0) & (earlier[..., None] == ranks)
    slots = jnp.einsum(
        "tkecrxm,tkecrd->tkecxmd",
        sender.astype(jnp.bfloat16),
        all_rows,
        preferred_element_type=jnp.float32,
    ).astype(jnp.bfloat16)
    gate_part = jnp.einsum("tkecxmd,xdf->tkecxmf", slots, w_gate, preferred_element_type=jnp.float32)
    up_part = jnp.einsum("tkecxmd,xdf->tkecxmf", slots, w_up, preferred_element_type=jnp.float32)
    hidden_act = ((up_part + 1.0) * gate_part * jax.nn.sigmoid(1.702 * gate_part)).astype(
        jnp.bfloat16
    )
    partial = jnp.einsum(
        "tkecxmf,xfd->tkecxmd", hidden_act, w_down, preferred_element_type=jnp.float32
    ).astype(jnp.bfloat16)
    weights = jnp.where(sender, gate_of[..., None], 0.0).astype(jnp.bfloat16)
    if local_experts * MOST < rows:
        terms = partial.astype(jnp.float32)
        spread = "tecrxm,tecxmd->tecrd"
    else:
        terms = jnp.einsum(
            "tkecrxm,tkecxmd->tkecrd", weights, partial, preferred_element_type=jnp.float32
        )
        spread = None
    terms = terms[0] + sibling(terms[1])
    terms = lax.psum_scatter(
        terms, "dp", scatter_dimension=0, tiled=True, axis_index_groups=same_core
    )[0]
    terms = lax.psum_scatter(terms, "expert", scatter_dimension=0, tiled=True)[0]
    if spread is not None:
        chip = lax.axis_index("dp") // 2
        own_weights = lax.dynamic_index_in_dim(weights[0], chip, 0, keepdims=False)
        own_weights = lax.dynamic_index_in_dim(own_weights, lax.axis_index("expert"), 0, keepdims=False)
        terms = jnp.einsum(
            "crxm,cxmd->crd",
            own_weights.astype(jnp.float32),
            terms,
            precision=lax.Precision.HIGHEST,
            preferred_element_type=jnp.float32,
        )
    own_now = lax.dynamic_index_in_dim(terms, core, 0, keepdims=False)
    own_other = sibling(lax.dynamic_index_in_dim(terms, 1 - core, 0, keepdims=False))
    branch_out = jnp.where(core == 0, jnp.stack([own_now, own_other]), jnp.stack([own_other, own_now]))
    return (residual + branch_out).astype(jnp.bfloat16)


def body(
    hidden,
    norm_gain,
    router,
    routes,
    w_gate,
    w_up,
    w_down,
    queries,
    new_key,
    new_value,
    key_pages,
    value_pages,
    page_counts,
    page_order,
):
    host_keys, host_values = (
        lax.all_to_all(key_pages, "dp", split_axis=0, concat_axis=0, tiled=True),
        lax.all_to_all(value_pages, "dp", split_axis=0, concat_axis=0, tiled=True),
    )
    kv_width = KV_HEADS * HEAD_DIM
    space_keys = host_keys.reshape(-1, BLOCK, kv_width)
    space_values = host_values.reshape(-1, BLOCK, kv_width)
    context = attention(
        queries, new_key, new_value, space_keys, space_values, page_counts[0], page_order[0]
    )
    layer_out = moe_layer(hidden, norm_gain, router, routes, w_gate, w_up, w_down)
    return (context, layer_out)


def solution(mesh):
    return jax.shard_map(
        body,
        mesh=mesh,
        in_specs=(
            P(None, ("dp", "expert"), None),
            P(),
            P(),
            P(None, ("dp", "expert"), None),
            P("expert", None, "dp"),
            P("expert", None, "dp"),
            P("expert", "dp", None),
            P(None, ("dp", "expert"), None),
            P(None, ("dp", "expert"), None),
            P(None, ("dp", "expert"), None),
            P(("dp", "expert"), None, None, None),
            P(("dp", "expert"), None, None, None),
            P(("dp", "expert"), None),
            P(("dp", "expert"), None),
        ),
        out_specs=(P(None, ("dp", "expert"), None), P(None, ("dp", "expert"), None)),
        check_vma=False,
    )
```

```python
import jax
import jax.numpy as jnp
from jax import lax
from jax.sharding import PartitionSpec as P

HEADS = 64
KV_HEADS = 8
HEAD_DIM = 64
EXPERTS = 64
MOST = 2
STEPS = 2
BLOCK = 16


def page_layout(counts, page_perm, most_pages):
    starts = jnp.cumsum(counts) - counts
    offsets = jnp.arange(most_pages, dtype=jnp.int32)
    places = starts[:, None] + offsets[None, :]
    places = jnp.where(offsets[None, :] < counts[:, None], places, 0)
    return jnp.take(page_perm, places, axis=0)


def attention(query_rows, fresh_keys, fresh_values, space_keys, space_values, counts, page_perm):
    group_size = HEADS // KV_HEADS
    most_pages = page_perm.shape[0] // 3
    row_count = counts.shape[0]
    cache_span = most_pages * BLOCK
    slot_ids = page_layout(counts, page_perm, most_pages).reshape(-1)
    cache_keys = jnp.take(space_keys, slot_ids, axis=0).reshape(
        row_count, cache_span, KV_HEADS, HEAD_DIM
    )
    cache_values = jnp.take(space_values, slot_ids, axis=0).reshape(
        row_count, cache_span, KV_HEADS, HEAD_DIM
    )
    live_mask = jnp.arange(cache_span)[None, :] < (counts * BLOCK)[:, None]
    query_heads = query_rows.reshape(STEPS, row_count, KV_HEADS, group_size, HEAD_DIM)
    new_keys = fresh_keys.reshape(STEPS, row_count, KV_HEADS, HEAD_DIM)
    new_values = fresh_values.reshape(STEPS, row_count, KV_HEADS, HEAD_DIM)
    score_scale = HEAD_DIM ** (-0.5)
    old_scores = (
        jnp.einsum("trkgh,rlkh->trkgl", query_heads, cache_keys, preferred_element_type=jnp.float32)
        * score_scale
    )
    old_scores = jnp.where(live_mask[None, :, None, None, :], old_scores, -jnp.inf)
    new_scores = (
        jnp.einsum("trkgh,urkh->trkgu", query_heads, new_keys, preferred_element_type=jnp.float32)
        * score_scale
    )
    causal = jnp.arange(STEPS)[None, :] <= jnp.arange(STEPS)[:, None]
    new_scores = jnp.where(causal[:, None, None, None, :], new_scores, -jnp.inf)
    row_max = jnp.maximum(jnp.max(old_scores, axis=-1), jnp.max(new_scores, axis=-1))
    old_probs = jnp.exp(old_scores - row_max[..., None])
    new_probs = jnp.exp(new_scores - row_max[..., None])
    denominator = jnp.sum(old_probs, axis=-1) + jnp.sum(new_probs, axis=-1)
    numerator = jnp.einsum(
        "trkgl,rlkh->trkgh",
        old_probs.astype(jnp.bfloat16),
        cache_values,
        preferred_element_type=jnp.float32,
    )
    numerator = numerator + jnp.einsum(
        "trkgu,urkh->trkgh",
        new_probs.astype(jnp.bfloat16),
        new_values,
        preferred_element_type=jnp.float32,
    )
    result = numerator / denominator[..., None]
    return result.reshape(STEPS, row_count, HEADS * HEAD_DIM).astype(jnp.bfloat16)


MOST = 2


def moe_layer(hidden, norm_gain, router, routes, w_gate, w_up, w_down):
    steps, rows, model_width = hidden.shape
    topk = routes.shape[-1]
    n_dp = lax.axis_size("dp")
    n_ex = lax.axis_size("expert")
    local_experts = w_gate.shape[0]
    blocks = n_dp * n_ex
    residual = hidden.astype(jnp.float32)
    scale_rows = lax.rsqrt(jnp.mean(residual * residual, axis=-1, keepdims=True) + 1e-05)
    normed = (residual * scale_rows * norm_gain).astype(jnp.bfloat16)
    logit_rows = jnp.einsum("trd,de->tre", normed, router, preferred_element_type=jnp.float32)
    chosen = jnp.take_along_axis(logit_rows, routes, axis=-1)
    spreads = chosen[..., None, :] - chosen[..., :, None]
    gate_vals = (1.0 / jnp.sum(jnp.exp(spreads), axis=-1)).astype(jnp.bfloat16)
    lanes = -(-(model_width + 2 * topk) // 128) * 128
    filler = jnp.zeros((steps, rows, lanes - model_width - 2 * topk), jnp.bfloat16)
    payload = jnp.concatenate(
        [normed, gate_vals, routes.astype(jnp.bfloat16), filler], axis=-1
    )
    gathered = lax.all_gather(payload, ("dp", "expert"), axis=1, tiled=False)
    return gathered, residual


def moe_finish(gathered, residual, topk, w_gate, w_up, w_down):
    steps, rows, model_width = residual.shape
    n_dp = lax.axis_size("dp")
    n_ex = lax.axis_size("expert")
    local_experts = w_gate.shape[0]
    all_rows = gathered[..., :model_width]
    all_gates = gathered[..., model_width : model_width + topk]
    all_ids = jnp.round(gathered[..., model_width + topk : model_width + 2 * topk]).astype(jnp.int32)
    first = lax.axis_index("expert") * local_experts
    numbers = first + jnp.arange(local_experts, dtype=jnp.int32)
    matches = all_ids[..., None] == numbers
    picked = jnp.any(matches, axis=-2).astype(jnp.int32)
    gate_of = jnp.sum(jnp.where(matches, all_gates[..., None].astype(jnp.float32), 0.0), axis=-2)
    earlier = jnp.cumsum(picked, axis=2) - picked
    ranks = jnp.arange(MOST, dtype=jnp.int32)
    sender = (picked[..., None] > 0) & (earlier[..., None] == ranks)
    slots = jnp.einsum(
        "tbrxm,tbrd->tbxmd",
        sender.astype(jnp.bfloat16),
        all_rows,
        preferred_element_type=jnp.float32,
    ).astype(jnp.bfloat16)
    gate_part = jnp.einsum("tbxmd,xdf->tbxmf", slots, w_gate, preferred_element_type=jnp.float32)
    up_part = jnp.einsum("tbxmd,xdf->tbxmf", slots, w_up, preferred_element_type=jnp.float32)
    hidden_act = ((up_part + 1.0) * gate_part * jax.nn.sigmoid(1.702 * gate_part)).astype(
        jnp.bfloat16
    )
    partial = jnp.einsum(
        "tbxmf,xfd->tbxmd", hidden_act, w_down, preferred_element_type=jnp.float32
    ).astype(jnp.bfloat16)
    weights = jnp.where(sender, gate_of[..., None], 0.0).astype(jnp.bfloat16)
    grid = (steps, n_dp, n_ex)
    if local_experts * MOST < rows:
        summed = lax.psum_scatter(
            partial.astype(jnp.float32).reshape(grid + partial.shape[2:]),
            "dp",
            scatter_dimension=1,
            tiled=True,
        )[:, 0]
        own = lax.axis_index("dp")
        own_weights = lax.dynamic_index_in_dim(weights.reshape(grid + weights.shape[2:]), own, 1, False)
        row_terms = jnp.einsum(
            "terxm,texmd->terd",
            own_weights.astype(jnp.float32),
            summed,
            precision=lax.Precision.HIGHEST,
            preferred_element_type=jnp.float32,
        )
    else:
        row_terms = jnp.einsum(
            "tbrxm,tbxmd->tbrd", weights, partial, preferred_element_type=jnp.float32
        ).astype(jnp.bfloat16)
        row_terms = lax.psum_scatter(
            row_terms.reshape(grid + row_terms.shape[2:]), "dp", scatter_dimension=1, tiled=True
        )[:, 0]
    branch_out = lax.psum_scatter(row_terms, "expert", scatter_dimension=1, tiled=True)
    return (residual + branch_out[:, 0].astype(jnp.float32)).astype(jnp.bfloat16)


def body(
    hidden,
    norm_gain,
    router,
    routes,
    w_gate,
    w_up,
    w_down,
    queries,
    new_key,
    new_value,
    key_pages,
    value_pages,
    page_counts,
    page_order,
):
    host_keys, host_values = (
        lax.all_to_all(key_pages, "dp", split_axis=0, concat_axis=0, tiled=True),
        lax.all_to_all(value_pages, "dp", split_axis=0, concat_axis=0, tiled=True),
    )
    kv_width = KV_HEADS * HEAD_DIM
    space_keys = host_keys.reshape(-1, BLOCK, kv_width)
    space_values = host_values.reshape(-1, BLOCK, kv_width)
    gathered, residual = moe_layer(hidden, norm_gain, router, routes, w_gate, w_up, w_down)
    context = attention(
        queries, new_key, new_value, space_keys, space_values, page_counts[0], page_order[0]
    )
    gathered, context = lax.optimization_barrier((gathered, context))
    layer_out = moe_finish(gathered, residual, routes.shape[-1], w_gate, w_up, w_down)
    return (context, layer_out)


def solution(mesh):
    return jax.shard_map(
        body,
        mesh=mesh,
        in_specs=(
            P(None, ("dp", "expert"), None),
            P(),
            P(),
            P(None, ("dp", "expert"), None),
            P("expert", None, "dp"),
            P("expert", None, "dp"),
            P("expert", "dp", None),
            P(None, ("dp", "expert"), None),
            P(None, ("dp", "expert"), None),
            P(None, ("dp", "expert"), None),
            P(("dp", "expert"), None, None, None),
            P(("dp", "expert"), None, None, None),
            P(("dp", "expert"), None),
            P(("dp", "expert"), None),
        ),
        out_specs=(P(None, ("dp", "expert"), None), P(None, ("dp", "expert"), None)),
        check_vma=False,
    )
```

```python
import jax
import jax.numpy as jnp
from jax import lax
from jax.sharding import PartitionSpec as P

HEADS = 64
KV_HEADS = 8
HEAD_DIM = 64
EXPERTS = 64
MOST = 2
STEPS = 2
BLOCK = 16


def page_layout(counts, page_perm, most_pages):
    starts = jnp.cumsum(counts) - counts
    offsets = jnp.arange(most_pages, dtype=jnp.int32)
    places = starts[:, None] + offsets[None, :]
    places = jnp.where(offsets[None, :] < counts[:, None], places, 0)
    return jnp.take(page_perm, places, axis=0)


def attention(query_rows, fresh_keys, fresh_values, space_keys, space_values, counts, page_perm):
    group_size = HEADS // KV_HEADS
    most_pages = page_perm.shape[0] // 3
    row_count = counts.shape[0]
    cache_span = most_pages * BLOCK
    slot_ids = page_layout(counts, page_perm, most_pages).reshape(-1)
    cache_keys = jnp.take(space_keys, slot_ids, axis=0).reshape(
        row_count, cache_span, KV_HEADS, HEAD_DIM
    )
    cache_values = jnp.take(space_values, slot_ids, axis=0).reshape(
        row_count, cache_span, KV_HEADS, HEAD_DIM
    )
    live_mask = jnp.arange(cache_span)[None, :] < (counts * BLOCK)[:, None]
    query_heads = query_rows.reshape(STEPS, row_count, KV_HEADS, group_size, HEAD_DIM)
    new_keys = fresh_keys.reshape(STEPS, row_count, KV_HEADS, HEAD_DIM)
    new_values = fresh_values.reshape(STEPS, row_count, KV_HEADS, HEAD_DIM)
    score_scale = HEAD_DIM ** (-0.5)
    old_scores = (
        jnp.einsum("trkgh,rlkh->trkgl", query_heads, cache_keys, preferred_element_type=jnp.float32)
        * score_scale
    )
    old_scores = jnp.where(live_mask[None, :, None, None, :], old_scores, -jnp.inf)
    new_scores = (
        jnp.einsum("trkgh,urkh->trkgu", query_heads, new_keys, preferred_element_type=jnp.float32)
        * score_scale
    )
    causal = jnp.arange(STEPS)[None, :] <= jnp.arange(STEPS)[:, None]
    new_scores = jnp.where(causal[:, None, None, None, :], new_scores, -jnp.inf)
    row_max = jnp.maximum(jnp.max(old_scores, axis=-1), jnp.max(new_scores, axis=-1))
    old_probs = jnp.exp(old_scores - row_max[..., None])
    new_probs = jnp.exp(new_scores - row_max[..., None])
    denominator = jnp.sum(old_probs, axis=-1) + jnp.sum(new_probs, axis=-1)
    numerator = jnp.einsum(
        "trkgl,rlkh->trkgh",
        old_probs.astype(jnp.bfloat16),
        cache_values,
        preferred_element_type=jnp.float32,
    )
    numerator = numerator + jnp.einsum(
        "trkgu,urkh->trkgh",
        new_probs.astype(jnp.bfloat16),
        new_values,
        preferred_element_type=jnp.float32,
    )
    result = numerator / denominator[..., None]
    return result.reshape(STEPS, row_count, HEADS * HEAD_DIM).astype(jnp.bfloat16)


MOST = 2


def moe_layer(hidden, norm_gain, router, routes, w_gate, w_up, w_down):
    steps, rows, model_width = hidden.shape
    topk = routes.shape[-1]
    n_dp = lax.axis_size("dp")
    n_ex = lax.axis_size("expert")
    local_experts = w_gate.shape[0]
    blocks = n_dp * n_ex
    residual = hidden.astype(jnp.float32)
    scale_rows = lax.rsqrt(jnp.mean(residual * residual, axis=-1, keepdims=True) + 1e-05)
    normed = (residual * scale_rows * norm_gain).astype(jnp.bfloat16)
    logit_rows = jnp.einsum("trd,de->tre", normed, router, preferred_element_type=jnp.float32)
    chosen = jnp.take_along_axis(logit_rows, routes, axis=-1)
    spreads = chosen[..., None, :] - chosen[..., :, None]
    gate_vals = (1.0 / jnp.sum(jnp.exp(spreads), axis=-1)).astype(jnp.bfloat16)
    lanes = -(-(model_width + 2 * topk) // 128) * 128
    filler = jnp.zeros((steps, rows, lanes - model_width - 2 * topk), jnp.bfloat16)
    payload = jnp.concatenate(
        [normed, gate_vals, routes.astype(jnp.bfloat16), filler], axis=-1
    )
    gathered = lax.all_gather(payload, ("dp", "expert"), axis=1, tiled=False)
    return gathered, residual


def moe_finish(gathered, residual, topk, w_gate, w_up, w_down):
    steps, rows, model_width = residual.shape
    n_dp = lax.axis_size("dp")
    n_ex = lax.axis_size("expert")
    local_experts = w_gate.shape[0]
    blocks = n_dp * n_ex
    all_rows = gathered[..., :model_width].reshape(steps * blocks * rows, model_width)
    all_gates = gathered[..., model_width : model_width + topk]
    all_ids = jnp.round(gathered[..., model_width + topk : model_width + 2 * topk]).astype(jnp.int32)
    first = lax.axis_index("expert") * local_experts
    numbers = first + jnp.arange(local_experts, dtype=jnp.int32)
    matches = all_ids[..., None] == numbers
    picked = jnp.any(matches, axis=-2).astype(jnp.int32)
    gate_of = jnp.sum(jnp.where(matches, all_gates[..., None].astype(jnp.float32), 0.0), axis=-2)
    earlier = jnp.cumsum(picked, axis=2) - picked
    ranks = jnp.arange(MOST, dtype=jnp.int32)
    sender = ((picked[..., None] > 0) & (earlier[..., None] == ranks)).astype(jnp.int32)
    row_no = jnp.arange(rows, dtype=jnp.int32)[:, None, None]
    slot_row = jnp.sum(sender * row_no, axis=2)
    slot_gate = jnp.sum(sender.astype(jnp.float32) * gate_of[..., None], axis=2)
    base = (jnp.arange(steps * blocks, dtype=jnp.int32) * rows).reshape(steps, blocks, 1, 1)
    slot_src = jnp.transpose(slot_row + base, (2, 0, 1, 3)).reshape(-1)
    slot_w = jnp.transpose(slot_gate, (2, 0, 1, 3)).reshape(-1).astype(jnp.bfloat16)
    slots = jnp.take(all_rows, slot_src, axis=0).reshape(local_experts, -1, model_width)
    gate_part = jnp.einsum("xsd,xdf->xsf", slots, w_gate, preferred_element_type=jnp.float32)
    up_part = jnp.einsum("xsd,xdf->xsf", slots, w_up, preferred_element_type=jnp.float32)
    hidden_act = ((up_part + 1.0) * gate_part * jax.nn.sigmoid(1.702 * gate_part)).astype(
        jnp.bfloat16
    )
    partial = jnp.einsum(
        "xsf,xfd->xsd", hidden_act, w_down, preferred_element_type=jnp.float32
    ).astype(jnp.bfloat16)
    partial = partial.reshape(-1, model_width)
    if local_experts * MOST < rows:
        slot_terms = partial.astype(jnp.float32).reshape(local_experts, steps, n_dp, n_ex, MOST, model_width)
        slot_terms = lax.psum_scatter(slot_terms, "dp", scatter_dimension=2, tiled=True)[:, :, 0]
        own = lax.axis_index("dp")
        own_sender = sender.reshape(steps, n_dp, n_ex, rows, local_experts, MOST)
        own_sender = lax.dynamic_index_in_dim(own_sender, own, 1, False)
        own_gate = lax.dynamic_index_in_dim(slot_gate.reshape(steps, n_dp, n_ex, local_experts, MOST), own, 1, False)
        own_weights = own_sender.astype(jnp.float32) * own_gate[:, :, None]
        row_terms = jnp.einsum(
            "terxm,xtemd->terd",
            own_weights,
            slot_terms,
            precision=lax.Precision.HIGHEST,
            preferred_element_type=jnp.float32,
        )
        branch_out = lax.psum_scatter(row_terms, "expert", scatter_dimension=1, tiled=True)[:, 0]
    else:
        q = jnp.arange(n_dp * n_ex * steps * rows, dtype=jnp.int32).reshape(n_dp, n_ex, steps, rows)
        q_src = (
            jnp.arange(steps, dtype=jnp.int32)[None, None, :, None] * (blocks * rows)
            + (jnp.arange(n_dp, dtype=jnp.int32)[:, None, None, None] * n_ex
               + jnp.arange(n_ex, dtype=jnp.int32)[None, :, None, None]) * rows
            + jnp.arange(rows, dtype=jnp.int32)[None, None, None, :]
        ) + 0 * q
        spread = jnp.where(
            slot_src[:, None] == q_src.reshape(1, -1),
            slot_w[:, None],
            jnp.zeros((), jnp.bfloat16),
        )
        row_terms = jnp.einsum("sq,sd->qd", spread, partial, preferred_element_type=jnp.float32)
        row_terms = row_terms.reshape(n_dp, n_ex, steps, rows, model_width)
        row_terms = lax.psum_scatter(row_terms, "dp", scatter_dimension=0, tiled=True)[0]
        branch_out = lax.psum_scatter(row_terms, "expert", scatter_dimension=0, tiled=True)[0]
    return (residual + branch_out).astype(jnp.bfloat16)


def body(
    hidden,
    norm_gain,
    router,
    routes,
    w_gate,
    w_up,
    w_down,
    queries,
    new_key,
    new_value,
    key_pages,
    value_pages,
    page_counts,
    page_order,
):
    host_keys, host_values = (
        lax.all_to_all(key_pages, "dp", split_axis=0, concat_axis=0, tiled=True),
        lax.all_to_all(value_pages, "dp", split_axis=0, concat_axis=0, tiled=True),
    )
    kv_width = KV_HEADS * HEAD_DIM
    space_keys = host_keys.reshape(-1, BLOCK, kv_width)
    space_values = host_values.reshape(-1, BLOCK, kv_width)
    gathered, residual = moe_layer(hidden, norm_gain, router, routes, w_gate, w_up, w_down)
    context = attention(
        queries, new_key, new_value, space_keys, space_values, page_counts[0], page_order[0]
    )
    gathered, context = lax.optimization_barrier((gathered, context))
    layer_out = moe_finish(gathered, residual, routes.shape[-1], w_gate, w_up, w_down)
    return (context, layer_out)


def solution(mesh):
    return jax.shard_map(
        body,
        mesh=mesh,
        in_specs=(
            P(None, ("dp", "expert"), None),
            P(),
            P(),
            P(None, ("dp", "expert"), None),
            P("expert", None, "dp"),
            P("expert", None, "dp"),
            P("expert", "dp", None),
            P(None, ("dp", "expert"), None),
            P(None, ("dp", "expert"), None),
            P(None, ("dp", "expert"), None),
            P(("dp", "expert"), None, None, None),
            P(("dp", "expert"), None, None, None),
            P(("dp", "expert"), None),
            P(("dp", "expert"), None),
        ),
        out_specs=(P(None, ("dp", "expert"), None), P(None, ("dp", "expert"), None)),
        check_vma=False,
    )
```

```python
import jax
import jax.numpy as jnp
from jax import lax
from jax.sharding import PartitionSpec as P

HEADS = 64
KV_HEADS = 8
HEAD_DIM = 64
EXPERTS = 64
MOST = 2
STEPS = 2
BLOCK = 16


def page_layout(counts, page_perm, most_pages):
    starts = jnp.cumsum(counts) - counts
    offsets = jnp.arange(most_pages, dtype=jnp.int32)
    places = starts[:, None] + offsets[None, :]
    places = jnp.where(offsets[None, :] < counts[:, None], places, 0)
    return jnp.take(page_perm, places, axis=0)


def attention(query_rows, fresh_keys, fresh_values, space_keys, space_values, counts, page_perm):
    group_size = HEADS // KV_HEADS
    most_pages = page_perm.shape[0] // 3
    row_count = counts.shape[0]
    cache_span = most_pages * BLOCK
    slot_ids = page_layout(counts, page_perm, most_pages).reshape(-1)
    cache_keys = jnp.take(space_keys, slot_ids, axis=0).reshape(
        row_count, cache_span, KV_HEADS, HEAD_DIM
    )
    cache_values = jnp.take(space_values, slot_ids, axis=0).reshape(
        row_count, cache_span, KV_HEADS, HEAD_DIM
    )
    live_mask = jnp.arange(cache_span)[None, :] < (counts * BLOCK)[:, None]
    query_heads = query_rows.reshape(STEPS, row_count, KV_HEADS, group_size, HEAD_DIM)
    new_keys = fresh_keys.reshape(STEPS, row_count, KV_HEADS, HEAD_DIM)
    new_values = fresh_values.reshape(STEPS, row_count, KV_HEADS, HEAD_DIM)
    score_scale = HEAD_DIM ** (-0.5)
    old_scores = (
        jnp.einsum("trkgh,rlkh->trkgl", query_heads, cache_keys, preferred_element_type=jnp.float32)
        * score_scale
    )
    old_scores = jnp.where(live_mask[None, :, None, None, :], old_scores, -jnp.inf)
    new_scores = (
        jnp.einsum("trkgh,urkh->trkgu", query_heads, new_keys, preferred_element_type=jnp.float32)
        * score_scale
    )
    causal = jnp.arange(STEPS)[None, :] <= jnp.arange(STEPS)[:, None]
    new_scores = jnp.where(causal[:, None, None, None, :], new_scores, -jnp.inf)
    row_max = jnp.maximum(jnp.max(old_scores, axis=-1), jnp.max(new_scores, axis=-1))
    old_probs = jnp.exp(old_scores - row_max[..., None])
    new_probs = jnp.exp(new_scores - row_max[..., None])
    denominator = jnp.sum(old_probs, axis=-1) + jnp.sum(new_probs, axis=-1)
    numerator = jnp.einsum(
        "trkgl,rlkh->trkgh",
        old_probs.astype(jnp.bfloat16),
        cache_values,
        preferred_element_type=jnp.float32,
    )
    numerator = numerator + jnp.einsum(
        "trkgu,urkh->trkgh",
        new_probs.astype(jnp.bfloat16),
        new_values,
        preferred_element_type=jnp.float32,
    )
    result = numerator / denominator[..., None]
    return result.reshape(STEPS, row_count, HEADS * HEAD_DIM).astype(jnp.bfloat16)


MOST = 2


def moe_layer(hidden, norm_gain, router, routes, w_gate, w_up, w_down):
    steps, rows, model_width = hidden.shape
    topk = routes.shape[-1]
    n_dp = lax.axis_size("dp")
    n_ex = lax.axis_size("expert")
    local_experts = w_gate.shape[0]
    blocks = n_dp * n_ex
    residual = hidden.astype(jnp.float32)
    scale_rows = lax.rsqrt(jnp.mean(residual * residual, axis=-1, keepdims=True) + 1e-05)
    normed = (residual * scale_rows * norm_gain).astype(jnp.bfloat16)
    logit_rows = jnp.einsum("trd,de->tre", normed, router, preferred_element_type=jnp.float32)
    chosen = jnp.take_along_axis(logit_rows, routes, axis=-1)
    spreads = chosen[..., None, :] - chosen[..., :, None]
    gate_vals = (1.0 / jnp.sum(jnp.exp(spreads), axis=-1)).astype(jnp.bfloat16)
    lanes = -(-(model_width + 2 * topk) // 128) * 128
    filler = jnp.zeros((steps, rows, lanes - model_width - 2 * topk), jnp.bfloat16)
    payload = jnp.concatenate(
        [normed, gate_vals, routes.astype(jnp.bfloat16), filler], axis=-1
    )
    gathered = lax.all_gather(payload, ("dp", "expert"), axis=1, tiled=False)
    return gathered, residual


def moe_finish(gathered, meta, residual, topk, w_gate, w_up, w_down):
    steps, rows, model_width = residual.shape
    n_dp = lax.axis_size("dp")
    n_ex = lax.axis_size("expert")
    local_experts = w_gate.shape[0]
    all_rows = gathered[..., :model_width]
    all_gates = meta[..., :topk]
    all_ids = jnp.round(meta[..., topk : 2 * topk]).astype(jnp.int32)
    first = lax.axis_index("expert") * local_experts
    numbers = first + jnp.arange(local_experts, dtype=jnp.int32)
    matches = all_ids[..., None] == numbers
    picked = jnp.any(matches, axis=-2).astype(jnp.int32)
    gate_of = jnp.sum(jnp.where(matches, all_gates[..., None].astype(jnp.float32), 0.0), axis=-2)
    earlier = jnp.cumsum(picked, axis=2) - picked
    ranks = jnp.arange(MOST, dtype=jnp.int32)
    sender = (picked[..., None] > 0) & (earlier[..., None] == ranks)
    groups = steps * n_dp * n_ex
    slot_count = local_experts * MOST
    sender_t = jnp.transpose(sender.reshape(groups, rows, slot_count), (0, 2, 1))
    slots = jnp.einsum(
        "gsr,grd->gsd",
        sender_t.astype(jnp.bfloat16),
        all_rows.reshape(groups, rows, model_width),
        preferred_element_type=jnp.float32,
    ).astype(jnp.bfloat16)
    slots = slots.reshape(steps, n_dp * n_ex, local_experts, MOST, model_width)
    gate_part = jnp.einsum("tbxmd,xdf->tbxmf", slots, w_gate, preferred_element_type=jnp.float32)
    up_part = jnp.einsum("tbxmd,xdf->tbxmf", slots, w_up, preferred_element_type=jnp.float32)
    hidden_act = ((up_part + 1.0) * gate_part * jax.nn.sigmoid(1.702 * gate_part)).astype(
        jnp.bfloat16
    )
    partial = jnp.einsum(
        "tbxmf,xfd->tbxmd", hidden_act, w_down, preferred_element_type=jnp.float32
    ).astype(jnp.bfloat16)
    weights = jnp.where(sender, gate_of[..., None], 0.0).astype(jnp.bfloat16)
    grid = (steps, n_dp, n_ex)
    if local_experts * MOST < rows:
        summed = lax.psum_scatter(
            partial.astype(jnp.float32).reshape(grid + partial.shape[2:]),
            "dp",
            scatter_dimension=1,
            tiled=True,
        )[:, 0]
        own = lax.axis_index("dp")
        own_weights = lax.dynamic_index_in_dim(weights.reshape(grid + weights.shape[2:]), own, 1, False)
        row_terms = jnp.einsum(
            "terxm,texmd->terd",
            own_weights.astype(jnp.float32),
            summed,
            precision=lax.Precision.HIGHEST,
            preferred_element_type=jnp.float32,
        )
    else:
        row_terms = jnp.einsum(
            "tbrxm,tbxmd->btrd", weights, partial, preferred_element_type=jnp.float32
        )
        row_terms = lax.psum_scatter(
            row_terms.reshape((n_dp, n_ex) + row_terms.shape[1:]), "dp", scatter_dimension=0, tiled=True
        )[0]
        row_terms = jnp.moveaxis(row_terms, 0, 1)
    branch_out = lax.psum_scatter(row_terms, "expert", scatter_dimension=1, tiled=True)
    return (residual + branch_out[:, 0]).astype(jnp.bfloat16)


def body(
    hidden,
    norm_gain,
    router,
    routes,
    w_gate,
    w_up,
    w_down,
    queries,
    new_key,
    new_value,
    key_pages,
    value_pages,
    page_counts,
    page_order,
):
    host_keys, host_values = (
        lax.all_to_all(key_pages, "dp", split_axis=0, concat_axis=0, tiled=True),
        lax.all_to_all(value_pages, "dp", split_axis=0, concat_axis=0, tiled=True),
    )
    kv_width = KV_HEADS * HEAD_DIM
    space_keys = host_keys.reshape(-1, BLOCK, kv_width)
    space_values = host_values.reshape(-1, BLOCK, kv_width)
    gathered, residual = moe_layer(hidden, norm_gain, router, routes, w_gate, w_up, w_down)
    context = attention(
        queries, new_key, new_value, space_keys, space_values, page_counts[0], page_order[0]
    )
    meta = gathered[..., hidden.shape[-1] :]
    gathered, meta, context = lax.optimization_barrier((gathered, meta, context))
    layer_out = moe_finish(gathered, meta, residual, routes.shape[-1], w_gate, w_up, w_down)
    return (context, layer_out)


def solution(mesh):
    return jax.shard_map(
        body,
        mesh=mesh,
        in_specs=(
            P(None, ("dp", "expert"), None),
            P(),
            P(),
            P(None, ("dp", "expert"), None),
            P("expert", None, "dp"),
            P("expert", None, "dp"),
            P("expert", "dp", None),
            P(None, ("dp", "expert"), None),
            P(None, ("dp", "expert"), None),
            P(None, ("dp", "expert"), None),
            P(("dp", "expert"), None, None, None),
            P(("dp", "expert"), None, None, None),
            P(("dp", "expert"), None),
            P(("dp", "expert"), None),
        ),
        out_specs=(P(None, ("dp", "expert"), None), P(None, ("dp", "expert"), None)),
        check_vma=False,
    )
```

```python
import jax
import jax.numpy as jnp
from jax import lax
from jax.sharding import PartitionSpec as P

HEADS = 64
KV_HEADS = 8
HEAD_DIM = 64
EXPERTS = 64
MOST = 2
STEPS = 2
BLOCK = 16


def page_layout(counts, page_perm, most_pages):
    starts = jnp.cumsum(counts) - counts
    offsets = jnp.arange(most_pages, dtype=jnp.int32)
    places = starts[:, None] + offsets[None, :]
    places = jnp.where(offsets[None, :] < counts[:, None], places, 0)
    return jnp.take(page_perm, places, axis=0)


def attention(query_rows, fresh_keys, fresh_values, space_keys, space_values, counts, page_perm):
    group_size = HEADS // KV_HEADS
    most_pages = page_perm.shape[0] // 3
    row_count = counts.shape[0]
    cache_span = most_pages * BLOCK
    slot_ids = page_layout(counts, page_perm, most_pages).reshape(-1)
    cache_keys = jnp.take(space_keys, slot_ids, axis=0).reshape(
        row_count, cache_span, KV_HEADS, HEAD_DIM
    )
    cache_values = jnp.take(space_values, slot_ids, axis=0).reshape(
        row_count, cache_span, KV_HEADS, HEAD_DIM
    )
    live_mask = jnp.arange(cache_span)[None, :] < (counts * BLOCK)[:, None]
    query_heads = query_rows.reshape(STEPS, row_count, KV_HEADS, group_size, HEAD_DIM)
    new_keys = fresh_keys.reshape(STEPS, row_count, KV_HEADS, HEAD_DIM)
    new_values = fresh_values.reshape(STEPS, row_count, KV_HEADS, HEAD_DIM)
    score_scale = HEAD_DIM ** (-0.5)
    old_scores = (
        jnp.einsum("trkgh,rlkh->trkgl", query_heads, cache_keys, preferred_element_type=jnp.float32)
        * score_scale
    )
    old_scores = jnp.where(live_mask[None, :, None, None, :], old_scores, -jnp.inf)
    new_scores = (
        jnp.einsum("trkgh,urkh->trkgu", query_heads, new_keys, preferred_element_type=jnp.float32)
        * score_scale
    )
    causal = jnp.arange(STEPS)[None, :] <= jnp.arange(STEPS)[:, None]
    new_scores = jnp.where(causal[:, None, None, None, :], new_scores, -jnp.inf)
    row_max = jnp.maximum(jnp.max(old_scores, axis=-1), jnp.max(new_scores, axis=-1))
    old_probs = jnp.exp(old_scores - row_max[..., None])
    new_probs = jnp.exp(new_scores - row_max[..., None])
    denominator = jnp.sum(old_probs, axis=-1) + jnp.sum(new_probs, axis=-1)
    numerator = jnp.einsum(
        "trkgl,rlkh->trkgh",
        old_probs.astype(jnp.bfloat16),
        cache_values,
        preferred_element_type=jnp.float32,
    )
    numerator = numerator + jnp.einsum(
        "trkgu,urkh->trkgh",
        new_probs.astype(jnp.bfloat16),
        new_values,
        preferred_element_type=jnp.float32,
    )
    result = numerator / denominator[..., None]
    return result.reshape(STEPS, row_count, HEADS * HEAD_DIM).astype(jnp.bfloat16)


MOST = 2


def moe_layer(hidden, norm_gain, router, routes, w_gate, w_up, w_down):
    steps, rows, model_width = hidden.shape
    topk = routes.shape[-1]
    n_dp = lax.axis_size("dp")
    n_ex = lax.axis_size("expert")
    local_experts = w_gate.shape[0]
    blocks = n_dp * n_ex
    residual = hidden.astype(jnp.float32)
    scale_rows = lax.rsqrt(jnp.mean(residual * residual, axis=-1, keepdims=True) + 1e-05)
    normed = (residual * scale_rows * norm_gain).astype(jnp.bfloat16)
    logit_rows = jnp.einsum("trd,de->tre", normed, router, preferred_element_type=jnp.float32)
    chosen = jnp.take_along_axis(logit_rows, routes, axis=-1)
    spreads = chosen[..., None, :] - chosen[..., :, None]
    gate_vals = (1.0 / jnp.sum(jnp.exp(spreads), axis=-1)).astype(jnp.bfloat16)
    lanes = -(-(model_width + 2 * topk) // 128) * 128
    filler = jnp.zeros((steps, rows, lanes - model_width - 2 * topk), jnp.bfloat16)
    payload = jnp.concatenate(
        [normed, gate_vals, routes.astype(jnp.bfloat16), filler], axis=-1
    )
    gathered = lax.all_gather(payload, ("dp", "expert"), axis=1, tiled=False)
    return gathered, residual


def moe_finish(gathered, meta, residual, topk, w_gate, w_up, w_down):
    steps, rows, model_width = residual.shape
    n_dp = lax.axis_size("dp")
    n_ex = lax.axis_size("expert")
    local_experts = w_gate.shape[0]
    all_rows = gathered[..., :model_width]
    all_gates = meta[..., :topk]
    all_ids = jnp.round(meta[..., topk : 2 * topk]).astype(jnp.int32)
    first = lax.axis_index("expert") * local_experts
    numbers = first + jnp.arange(local_experts, dtype=jnp.int32)
    matches = all_ids[..., None] == numbers
    picked = jnp.any(matches, axis=-2).astype(jnp.int32)
    gate_of = jnp.sum(jnp.where(matches, all_gates[..., None].astype(jnp.float32), 0.0), axis=-2)
    earlier = jnp.cumsum(picked, axis=2) - picked
    ranks = jnp.arange(MOST, dtype=jnp.int32)
    sender = (picked[..., None] > 0) & (earlier[..., None] == ranks)
    slots = jnp.einsum(
        "tbrxm,tbrd->tbxmd",
        sender.astype(jnp.bfloat16),
        all_rows,
        preferred_element_type=jnp.float32,
    ).astype(jnp.bfloat16)
    gate_part = jnp.einsum("tbxmd,xdf->tbxmf", slots, w_gate, preferred_element_type=jnp.float32)
    up_part = jnp.einsum("tbxmd,xdf->tbxmf", slots, w_up, preferred_element_type=jnp.float32)
    hidden_act = ((up_part + 1.0) * gate_part * jax.nn.sigmoid(1.702 * gate_part)).astype(
        jnp.bfloat16
    )
    partial = jnp.einsum(
        "tbxmf,xfd->tbxmd", hidden_act, w_down, preferred_element_type=jnp.float32
    ).astype(jnp.bfloat16)
    weights = jnp.where(sender, gate_of[..., None], 0.0).astype(jnp.bfloat16)
    grid = (steps, n_dp, n_ex)
    if local_experts * MOST < rows:
        summed = lax.psum_scatter(
            partial.astype(jnp.float32).reshape(grid + partial.shape[2:]),
            "dp",
            scatter_dimension=1,
            tiled=True,
        )[:, 0]
        own = lax.axis_index("dp")
        own_weights = lax.dynamic_index_in_dim(weights.reshape(grid + weights.shape[2:]), own, 1, False)
        row_terms = jnp.einsum(
            "terxm,texmd->terd",
            own_weights.astype(jnp.float32),
            summed,
            precision=lax.Precision.HIGHEST,
            preferred_element_type=jnp.float32,
        )
    else:
        row_terms = jnp.einsum(
            "tbrxm,tbxmd->btrd", weights, partial, preferred_element_type=jnp.float32
        ).astype(jnp.bfloat16)
        row_terms = lax.psum_scatter(
            row_terms.reshape((n_dp, n_ex) + row_terms.shape[1:]), "dp", scatter_dimension=0, tiled=True
        )[0]
        row_terms = jnp.moveaxis(row_terms, 0, 1)
    branch_out = lax.psum_scatter(row_terms, "expert", scatter_dimension=1, tiled=True)
    return (residual + branch_out[:, 0].astype(jnp.float32)).astype(jnp.bfloat16)


def body(
    hidden,
    norm_gain,
    router,
    routes,
    w_gate,
    w_up,
    w_down,
    queries,
    new_key,
    new_value,
    key_pages,
    value_pages,
    page_counts,
    page_order,
):
    host_keys, host_values = (
        lax.all_to_all(key_pages, "dp", split_axis=0, concat_axis=0, tiled=True),
        lax.all_to_all(value_pages, "dp", split_axis=0, concat_axis=0, tiled=True),
    )
    kv_width = KV_HEADS * HEAD_DIM
    space_keys = host_keys.reshape(-1, BLOCK, kv_width)
    space_values = host_values.reshape(-1, BLOCK, kv_width)
    gathered, residual = moe_layer(hidden, norm_gain, router, routes, w_gate, w_up, w_down)
    context = attention(
        queries, new_key, new_value, space_keys, space_values, page_counts[0], page_order[0]
    )
    meta = gathered[..., hidden.shape[-1] :]
    gathered, meta, context = lax.optimization_barrier((gathered, meta, context))
    layer_out = moe_finish(gathered, meta, residual, routes.shape[-1], w_gate, w_up, w_down)
    return (context, layer_out)


def solution(mesh):
    return jax.shard_map(
        body,
        mesh=mesh,
        in_specs=(
            P(None, ("dp", "expert"), None),
            P(),
            P(),
            P(None, ("dp", "expert"), None),
            P("expert", None, "dp"),
            P("expert", None, "dp"),
            P("expert", "dp", None),
            P(None, ("dp", "expert"), None),
            P(None, ("dp", "expert"), None),
            P(None, ("dp", "expert"), None),
            P(("dp", "expert"), None, None, None),
            P(("dp", "expert"), None, None, None),
            P(("dp", "expert"), None),
            P(("dp", "expert"), None),
        ),
        out_specs=(P(None, ("dp", "expert"), None), P(None, ("dp", "expert"), None)),
        check_vma=False,
    )
```

```python
import jax
import jax.numpy as jnp
from jax import lax
from jax.sharding import PartitionSpec as P

HEADS = 64
KV_HEADS = 8
HEAD_DIM = 64
EXPERTS = 64
MOST = 2
STEPS = 2
BLOCK = 16


def page_layout(counts, page_perm, most_pages):
    starts = jnp.cumsum(counts) - counts
    offsets = jnp.arange(most_pages, dtype=jnp.int32)
    places = starts[:, None] + offsets[None, :]
    places = jnp.where(offsets[None, :] < counts[:, None], places, 0)
    return jnp.take(page_perm, places, axis=0)


def attention(query_rows, fresh_keys, fresh_values, space_keys, space_values, counts, page_perm):
    group_size = HEADS // KV_HEADS
    most_pages = page_perm.shape[0] // 3
    row_count = counts.shape[0]
    cache_span = most_pages * BLOCK
    slot_ids = page_layout(counts, page_perm, most_pages).reshape(-1)
    cache_keys = jnp.take(space_keys, slot_ids, axis=0).reshape(
        row_count, cache_span, KV_HEADS, HEAD_DIM
    )
    cache_values = jnp.take(space_values, slot_ids, axis=0).reshape(
        row_count, cache_span, KV_HEADS, HEAD_DIM
    )
    live_mask = jnp.arange(cache_span)[None, :] < (counts * BLOCK)[:, None]
    query_heads = query_rows.reshape(STEPS, row_count, KV_HEADS, group_size, HEAD_DIM)
    new_keys = fresh_keys.reshape(STEPS, row_count, KV_HEADS, HEAD_DIM)
    new_values = fresh_values.reshape(STEPS, row_count, KV_HEADS, HEAD_DIM)
    score_scale = HEAD_DIM ** (-0.5)
    old_scores = (
        jnp.einsum("trkgh,rlkh->trkgl", query_heads, cache_keys, preferred_element_type=jnp.float32)
        * score_scale
    )
    old_scores = jnp.where(live_mask[None, :, None, None, :], old_scores, -jnp.inf)
    new_scores = (
        jnp.einsum("trkgh,urkh->trkgu", query_heads, new_keys, preferred_element_type=jnp.float32)
        * score_scale
    )
    causal = jnp.arange(STEPS)[None, :] <= jnp.arange(STEPS)[:, None]
    new_scores = jnp.where(causal[:, None, None, None, :], new_scores, -jnp.inf)
    row_max = jnp.maximum(jnp.max(old_scores, axis=-1), jnp.max(new_scores, axis=-1))
    old_probs = jnp.exp(old_scores - row_max[..., None])
    new_probs = jnp.exp(new_scores - row_max[..., None])
    denominator = jnp.sum(old_probs, axis=-1) + jnp.sum(new_probs, axis=-1)
    numerator = jnp.einsum(
        "trkgl,rlkh->trkgh",
        old_probs.astype(jnp.bfloat16),
        cache_values,
        preferred_element_type=jnp.float32,
    )
    numerator = numerator + jnp.einsum(
        "trkgu,urkh->trkgh",
        new_probs.astype(jnp.bfloat16),
        new_values,
        preferred_element_type=jnp.float32,
    )
    result = numerator / denominator[..., None]
    return result.reshape(STEPS, row_count, HEADS * HEAD_DIM).astype(jnp.bfloat16)


MOST = 2


def moe_layer(hidden, norm_gain, router, routes, w_gate, w_up, w_down):
    steps, rows, model_width = hidden.shape
    topk = routes.shape[-1]
    n_dp = lax.axis_size("dp")
    n_ex = lax.axis_size("expert")
    local_experts = w_gate.shape[0]
    blocks = n_dp * n_ex
    residual = hidden.astype(jnp.float32)
    scale_rows = lax.rsqrt(jnp.mean(residual * residual, axis=-1, keepdims=True) + 1e-05)
    normed = (residual * scale_rows * norm_gain).astype(jnp.bfloat16)
    logit_rows = jnp.einsum("trd,de->tre", normed, router, preferred_element_type=jnp.float32)
    chosen = jnp.take_along_axis(logit_rows, routes, axis=-1)
    spreads = chosen[..., None, :] - chosen[..., :, None]
    gate_vals = (1.0 / jnp.sum(jnp.exp(spreads), axis=-1)).astype(jnp.bfloat16)
    lanes = -(-(model_width + 2 * topk) // 128) * 128
    filler = jnp.zeros((steps, rows, lanes - model_width - 2 * topk), jnp.bfloat16)
    payload = jnp.concatenate(
        [normed, gate_vals, routes.astype(jnp.bfloat16), filler], axis=-1
    )
    gathered = lax.all_gather(payload, ("dp", "expert"), axis=1, tiled=False)
    return gathered, residual


def sibling(x):
    n_dp = lax.axis_size("dp")
    return lax.ppermute(x, "dp", perm=[(i, i ^ 1) for i in range(n_dp)])


def moe_finish(gathered, meta, residual, topk, w_gate, w_up, w_down):
    steps, rows, model_width = residual.shape
    n_dp = lax.axis_size("dp")
    n_ex = lax.axis_size("expert")
    local_experts = w_gate.shape[0]
    all_rows = gathered[..., :model_width]
    all_gates = meta[..., :topk]
    all_ids = jnp.round(meta[..., topk : 2 * topk]).astype(jnp.int32)
    first = lax.axis_index("expert") * local_experts
    numbers = first + jnp.arange(local_experts, dtype=jnp.int32)
    matches = all_ids[..., None] == numbers
    picked = jnp.any(matches, axis=-2).astype(jnp.int32)
    gate_of = jnp.sum(jnp.where(matches, all_gates[..., None].astype(jnp.float32), 0.0), axis=-2)
    earlier = jnp.cumsum(picked, axis=2) - picked
    ranks = jnp.arange(MOST, dtype=jnp.int32)
    sender = (picked[..., None] > 0) & (earlier[..., None] == ranks)
    slots = jnp.einsum(
        "tbrxm,tbrd->tbxmd",
        sender.astype(jnp.bfloat16),
        all_rows,
        preferred_element_type=jnp.float32,
    ).astype(jnp.bfloat16)
    gate_part = jnp.einsum("tbxmd,xdf->tbxmf", slots, w_gate, preferred_element_type=jnp.float32)
    up_part = jnp.einsum("tbxmd,xdf->tbxmf", slots, w_up, preferred_element_type=jnp.float32)
    hidden_act = ((up_part + 1.0) * gate_part * jax.nn.sigmoid(1.702 * gate_part)).astype(
        jnp.bfloat16
    )
    partial = jnp.einsum(
        "tbxmf,xfd->tbxmd", hidden_act, w_down, preferred_element_type=jnp.float32
    ).astype(jnp.bfloat16)
    weights = jnp.where(sender, gate_of[..., None], 0.0).astype(jnp.bfloat16)
    grid = (steps, n_dp, n_ex)
    if local_experts * MOST < rows:
        summed = lax.psum_scatter(
            partial.astype(jnp.float32).reshape(grid + partial.shape[2:]),
            "dp",
            scatter_dimension=1,
            tiled=True,
        )[:, 0]
        own = lax.axis_index("dp")
        own_weights = lax.dynamic_index_in_dim(weights.reshape(grid + weights.shape[2:]), own, 1, False)
        row_terms = jnp.einsum(
            "terxm,texmd->terd",
            own_weights.astype(jnp.float32),
            summed,
            precision=lax.Precision.HIGHEST,
            preferred_element_type=jnp.float32,
        )
    else:
        row_terms = jnp.einsum(
            "tbrxm,tbxmd->btrd", weights, partial, preferred_element_type=jnp.float32
        )
        chips = n_dp // 2
        core = lax.axis_index("dp") % 2
        same_core = [[i for i in range(n_dp) if i % 2 == c] for c in range(2)]
        row_terms = row_terms.reshape((chips, 2, n_ex) + row_terms.shape[1:])
        keep = lax.dynamic_index_in_dim(row_terms, core, 3, keepdims=False)
        give = lax.dynamic_index_in_dim(row_terms, 1 - core, 3, keepdims=False)
        chip_sum = (keep + sibling(give)).astype(jnp.bfloat16)
        chip_sum = lax.psum_scatter(
            chip_sum, "dp", scatter_dimension=0, tiled=True, axis_index_groups=same_core
        )[0]
        chip_sum = jnp.moveaxis(chip_sum, 1, 0)
        chip_sum = lax.psum_scatter(chip_sum, "expert", scatter_dimension=0, tiled=True)[0]
        mine = lax.dynamic_index_in_dim(chip_sum, core, 0, keepdims=False)
        theirs = sibling(lax.dynamic_index_in_dim(chip_sum, 1 - core, 0, keepdims=False))
        branch = jnp.where(core == 0, jnp.stack([mine, theirs]), jnp.stack([theirs, mine]))
        return (residual + branch.astype(jnp.float32)).astype(jnp.bfloat16)
    branch_out = lax.psum_scatter(row_terms, "expert", scatter_dimension=1, tiled=True)
    return (residual + branch_out[:, 0]).astype(jnp.bfloat16)


def body(
    hidden,
    norm_gain,
    router,
    routes,
    w_gate,
    w_up,
    w_down,
    queries,
    new_key,
    new_value,
    key_pages,
    value_pages,
    page_counts,
    page_order,
):
    host_keys, host_values = (
        lax.all_to_all(key_pages, "dp", split_axis=0, concat_axis=0, tiled=True),
        lax.all_to_all(value_pages, "dp", split_axis=0, concat_axis=0, tiled=True),
    )
    kv_width = KV_HEADS * HEAD_DIM
    space_keys = host_keys.reshape(-1, BLOCK, kv_width)
    space_values = host_values.reshape(-1, BLOCK, kv_width)
    gathered, residual = moe_layer(hidden, norm_gain, router, routes, w_gate, w_up, w_down)
    context = attention(
        queries, new_key, new_value, space_keys, space_values, page_counts[0], page_order[0]
    )
    meta = gathered[..., hidden.shape[-1] :]
    gathered, meta, context = lax.optimization_barrier((gathered, meta, context))
    layer_out = moe_finish(gathered, meta, residual, routes.shape[-1], w_gate, w_up, w_down)
    return (context, layer_out)


def solution(mesh):
    return jax.shard_map(
        body,
        mesh=mesh,
        in_specs=(
            P(None, ("dp", "expert"), None),
            P(),
            P(),
            P(None, ("dp", "expert"), None),
            P("expert", None, "dp"),
            P("expert", None, "dp"),
            P("expert", "dp", None),
            P(None, ("dp", "expert"), None),
            P(None, ("dp", "expert"), None),
            P(None, ("dp", "expert"), None),
            P(("dp", "expert"), None, None, None),
            P(("dp", "expert"), None, None, None),
            P(("dp", "expert"), None),
            P(("dp", "expert"), None),
        ),
        out_specs=(P(None, ("dp", "expert"), None), P(None, ("dp", "expert"), None)),
        check_vma=False,
    )
```

```python
import jax
import jax.numpy as jnp
from jax import lax
from jax.sharding import PartitionSpec as P

HEADS = 64
KV_HEADS = 8
HEAD_DIM = 64
EXPERTS = 64
MOST = 2
STEPS = 2
BLOCK = 16


def page_layout(counts, page_perm, most_pages):
    starts = jnp.cumsum(counts) - counts
    offsets = jnp.arange(most_pages, dtype=jnp.int32)
    places = starts[:, None] + offsets[None, :]
    places = jnp.where(offsets[None, :] < counts[:, None], places, 0)
    return jnp.take(page_perm, places, axis=0)


def attention(query_rows, fresh_keys, fresh_values, space_keys, space_values, counts, page_perm):
    group_size = HEADS // KV_HEADS
    most_pages = page_perm.shape[0] // 3
    row_count = counts.shape[0]
    cache_span = most_pages * BLOCK
    slot_ids = page_layout(counts, page_perm, most_pages).reshape(-1)
    cache_keys = jnp.take(space_keys, slot_ids, axis=0).reshape(
        row_count, cache_span, KV_HEADS, HEAD_DIM
    )
    cache_values = jnp.take(space_values, slot_ids, axis=0).reshape(
        row_count, cache_span, KV_HEADS, HEAD_DIM
    )
    live_mask = jnp.arange(cache_span)[None, :] < (counts * BLOCK)[:, None]
    query_heads = query_rows.reshape(STEPS, row_count, KV_HEADS, group_size, HEAD_DIM)
    new_keys = fresh_keys.reshape(STEPS, row_count, KV_HEADS, HEAD_DIM)
    new_values = fresh_values.reshape(STEPS, row_count, KV_HEADS, HEAD_DIM)
    score_scale = HEAD_DIM ** (-0.5)
    old_scores = (
        jnp.einsum("trkgh,rlkh->trkgl", query_heads, cache_keys, preferred_element_type=jnp.float32)
        * score_scale
    )
    old_scores = jnp.where(live_mask[None, :, None, None, :], old_scores, -jnp.inf)
    new_scores = (
        jnp.einsum("trkgh,urkh->trkgu", query_heads, new_keys, preferred_element_type=jnp.float32)
        * score_scale
    )
    causal = jnp.arange(STEPS)[None, :] <= jnp.arange(STEPS)[:, None]
    new_scores = jnp.where(causal[:, None, None, None, :], new_scores, -jnp.inf)
    row_max = jnp.maximum(jnp.max(old_scores, axis=-1), jnp.max(new_scores, axis=-1))
    old_probs = jnp.exp(old_scores - row_max[..., None])
    new_probs = jnp.exp(new_scores - row_max[..., None])
    denominator = jnp.sum(old_probs, axis=-1) + jnp.sum(new_probs, axis=-1)
    numerator = jnp.einsum(
        "trkgl,rlkh->trkgh",
        old_probs.astype(jnp.bfloat16),
        cache_values,
        preferred_element_type=jnp.float32,
    )
    numerator = numerator + jnp.einsum(
        "trkgu,urkh->trkgh",
        new_probs.astype(jnp.bfloat16),
        new_values,
        preferred_element_type=jnp.float32,
    )
    result = numerator / denominator[..., None]
    return result.reshape(STEPS, row_count, HEADS * HEAD_DIM).astype(jnp.bfloat16)


MOST = 2


def moe_layer(hidden, norm_gain, router, routes, w_gate, w_up, w_down):
    steps, rows, model_width = hidden.shape
    topk = routes.shape[-1]
    n_dp = lax.axis_size("dp")
    n_ex = lax.axis_size("expert")
    local_experts = w_gate.shape[0]
    blocks = n_dp * n_ex
    residual = hidden.astype(jnp.float32)
    scale_rows = lax.rsqrt(jnp.mean(residual * residual, axis=-1, keepdims=True) + 1e-05)
    normed = (residual * scale_rows * norm_gain).astype(jnp.bfloat16)
    logit_rows = jnp.einsum("trd,de->tre", normed, router, preferred_element_type=jnp.float32)
    chosen = jnp.take_along_axis(logit_rows, routes, axis=-1)
    spreads = chosen[..., None, :] - chosen[..., :, None]
    gate_vals = (1.0 / jnp.sum(jnp.exp(spreads), axis=-1)).astype(jnp.bfloat16)
    lanes = -(-(model_width + 2 * topk) // 128) * 128
    filler = jnp.zeros((steps, rows, lanes - model_width - 2 * topk), jnp.bfloat16)
    payload = jnp.concatenate(
        [normed, gate_vals, routes.astype(jnp.bfloat16), filler], axis=-1
    )
    gathered = lax.all_gather(payload, ("dp", "expert"), axis=1, tiled=False)
    return gathered, residual


def moe_finish(gathered, meta, residual, topk, w_gate, w_up, w_down):
    steps, rows, model_width = residual.shape
    n_dp = lax.axis_size("dp")
    n_ex = lax.axis_size("expert")
    local_experts = w_gate.shape[0]
    all_rows = gathered[..., :model_width]
    all_gates = meta[..., :topk]
    all_ids = jnp.round(meta[..., topk : 2 * topk]).astype(jnp.int32)
    first = lax.axis_index("expert") * local_experts
    numbers = first + jnp.arange(local_experts, dtype=jnp.int32)
    matches = all_ids[..., None] == numbers
    picked = jnp.any(matches, axis=-2).astype(jnp.int32)
    gate_of = jnp.sum(jnp.where(matches, all_gates[..., None].astype(jnp.float32), 0.0), axis=-2)
    earlier = jnp.cumsum(picked, axis=2) - picked
    ranks = jnp.arange(MOST, dtype=jnp.int32)
    sender = (picked[..., None] > 0) & (earlier[..., None] == ranks)
    slots = jnp.einsum(
        "tbrxm,tbrd->tbxmd",
        sender.astype(jnp.bfloat16),
        all_rows,
        preferred_element_type=jnp.float32,
    ).astype(jnp.bfloat16)
    gate_part = jnp.einsum("tbxmd,xdf->tbxmf", slots, w_gate, preferred_element_type=jnp.float32)
    up_part = jnp.einsum("tbxmd,xdf->tbxmf", slots, w_up, preferred_element_type=jnp.float32)
    hidden_act = ((up_part + 1.0) * gate_part * jax.nn.sigmoid(1.702 * gate_part)).astype(
        jnp.bfloat16
    )
    partial = jnp.einsum(
        "tbxmf,xfd->tbxmd", hidden_act, w_down, preferred_element_type=jnp.float32
    ).astype(jnp.bfloat16)
    weights = jnp.where(sender, gate_of[..., None], 0.0).astype(jnp.bfloat16)
    grid = (steps, n_dp, n_ex)
    if local_experts * MOST < rows:
        summed = lax.psum_scatter(
            partial.astype(jnp.float32).reshape(grid + partial.shape[2:]),
            "dp",
            scatter_dimension=1,
            tiled=True,
        )[:, 0]
        own = lax.axis_index("dp")
        own_weights = lax.dynamic_index_in_dim(weights.reshape(grid + weights.shape[2:]), own, 1, False)
        row_terms = jnp.einsum(
            "terxm,texmd->terd",
            own_weights.astype(jnp.float32),
            summed,
            precision=lax.Precision.HIGHEST,
            preferred_element_type=jnp.float32,
        )
    else:
        row_terms = jnp.einsum(
            "tbrxm,tbxmd->btrd", weights, partial, preferred_element_type=jnp.float32
        ).astype(jnp.bfloat16)
        branch_out = lax.psum_scatter(row_terms, ("dp", "expert"), scatter_dimension=0, tiled=True)
        return (residual + branch_out[0].astype(jnp.float32)).astype(jnp.bfloat16)
    branch_out = lax.psum_scatter(row_terms, "expert", scatter_dimension=1, tiled=True)
    return (residual + branch_out[:, 0].astype(jnp.float32)).astype(jnp.bfloat16)


def body(
    hidden,
    norm_gain,
    router,
    routes,
    w_gate,
    w_up,
    w_down,
    queries,
    new_key,
    new_value,
    key_pages,
    value_pages,
    page_counts,
    page_order,
):
    host_keys, host_values = (
        lax.all_to_all(key_pages, "dp", split_axis=0, concat_axis=0, tiled=True),
        lax.all_to_all(value_pages, "dp", split_axis=0, concat_axis=0, tiled=True),
    )
    kv_width = KV_HEADS * HEAD_DIM
    space_keys = host_keys.reshape(-1, BLOCK, kv_width)
    space_values = host_values.reshape(-1, BLOCK, kv_width)
    gathered, residual = moe_layer(hidden, norm_gain, router, routes, w_gate, w_up, w_down)
    context = attention(
        queries, new_key, new_value, space_keys, space_values, page_counts[0], page_order[0]
    )
    meta = gathered[..., hidden.shape[-1] :]
    gathered, meta, context = lax.optimization_barrier((gathered, meta, context))
    layer_out = moe_finish(gathered, meta, residual, routes.shape[-1], w_gate, w_up, w_down)
    return (context, layer_out)


def solution(mesh):
    return jax.shard_map(
        body,
        mesh=mesh,
        in_specs=(
            P(None, ("dp", "expert"), None),
            P(),
            P(),
            P(None, ("dp", "expert"), None),
            P("expert", None, "dp"),
            P("expert", None, "dp"),
            P("expert", "dp", None),
            P(None, ("dp", "expert"), None),
            P(None, ("dp", "expert"), None),
            P(None, ("dp", "expert"), None),
            P(("dp", "expert"), None, None, None),
            P(("dp", "expert"), None, None, None),
            P(("dp", "expert"), None),
            P(("dp", "expert"), None),
        ),
        out_specs=(P(None, ("dp", "expert"), None), P(None, ("dp", "expert"), None)),
        check_vma=False,
    )
```

```python
import jax
import jax.numpy as jnp
from jax import lax
from jax.sharding import PartitionSpec as P

HEADS = 64
KV_HEADS = 8
HEAD_DIM = 64
EXPERTS = 64
MOST = 2
STEPS = 2
BLOCK = 16


def page_layout(counts, page_perm, most_pages):
    starts = jnp.cumsum(counts) - counts
    offsets = jnp.arange(most_pages, dtype=jnp.int32)
    places = starts[:, None] + offsets[None, :]
    places = jnp.where(offsets[None, :] < counts[:, None], places, 0)
    return jnp.take(page_perm, places, axis=0)


def attention(query_rows, fresh_keys, fresh_values, space_keys, space_values, counts, page_perm):
    group_size = HEADS // KV_HEADS
    most_pages = page_perm.shape[0] // 3
    row_count = counts.shape[0]
    cache_span = most_pages * BLOCK
    slot_ids = page_layout(counts, page_perm, most_pages).reshape(-1)
    cache_keys = jnp.take(space_keys, slot_ids, axis=0).reshape(
        row_count, cache_span, KV_HEADS, HEAD_DIM
    )
    cache_values = jnp.take(space_values, slot_ids, axis=0).reshape(
        row_count, cache_span, KV_HEADS, HEAD_DIM
    )
    live_mask = jnp.arange(cache_span)[None, :] < (counts * BLOCK)[:, None]
    query_heads = query_rows.reshape(STEPS, row_count, KV_HEADS, group_size, HEAD_DIM)
    new_keys = fresh_keys.reshape(STEPS, row_count, KV_HEADS, HEAD_DIM)
    new_values = fresh_values.reshape(STEPS, row_count, KV_HEADS, HEAD_DIM)
    score_scale = HEAD_DIM ** (-0.5)
    old_scores = (
        jnp.einsum("trkgh,rlkh->trkgl", query_heads, cache_keys, preferred_element_type=jnp.float32)
        * score_scale
    )
    old_scores = jnp.where(live_mask[None, :, None, None, :], old_scores, -jnp.inf)
    new_scores = (
        jnp.einsum("trkgh,urkh->trkgu", query_heads, new_keys, preferred_element_type=jnp.float32)
        * score_scale
    )
    causal = jnp.arange(STEPS)[None, :] <= jnp.arange(STEPS)[:, None]
    new_scores = jnp.where(causal[:, None, None, None, :], new_scores, -jnp.inf)
    row_max = jnp.maximum(jnp.max(old_scores, axis=-1), jnp.max(new_scores, axis=-1))
    old_probs = jnp.exp(old_scores - row_max[..., None])
    new_probs = jnp.exp(new_scores - row_max[..., None])
    denominator = jnp.sum(old_probs, axis=-1) + jnp.sum(new_probs, axis=-1)
    numerator = jnp.einsum(
        "trkgl,rlkh->trkgh",
        old_probs.astype(jnp.bfloat16),
        cache_values,
        preferred_element_type=jnp.float32,
    )
    numerator = numerator + jnp.einsum(
        "trkgu,urkh->trkgh",
        new_probs.astype(jnp.bfloat16),
        new_values,
        preferred_element_type=jnp.float32,
    )
    result = numerator / denominator[..., None]
    return result.reshape(STEPS, row_count, HEADS * HEAD_DIM).astype(jnp.bfloat16)


MOST = 2


def moe_layer(hidden, norm_gain, router, routes, w_gate, w_up, w_down):
    steps, rows, model_width = hidden.shape
    topk = routes.shape[-1]
    n_dp = lax.axis_size("dp")
    n_ex = lax.axis_size("expert")
    local_experts = w_gate.shape[0]
    blocks = n_dp * n_ex
    residual = hidden.astype(jnp.float32)
    scale_rows = lax.rsqrt(jnp.mean(residual * residual, axis=-1, keepdims=True) + 1e-05)
    normed = (residual * scale_rows * norm_gain).astype(jnp.bfloat16)
    logit_rows = jnp.einsum("trd,de->tre", normed, router, preferred_element_type=jnp.float32)
    chosen = jnp.take_along_axis(logit_rows, routes, axis=-1)
    spreads = chosen[..., None, :] - chosen[..., :, None]
    gate_vals = (1.0 / jnp.sum(jnp.exp(spreads), axis=-1)).astype(jnp.bfloat16)
    lanes = -(-(model_width + 2 * topk) // 128) * 128
    filler = jnp.zeros((steps, rows, lanes - model_width - 2 * topk), jnp.bfloat16)
    payload = jnp.concatenate(
        [normed, gate_vals, routes.astype(jnp.bfloat16), filler], axis=-1
    )
    gathered = [
        lax.all_gather(payload[t : t + 1], ("dp", "expert"), axis=1, tiled=False)
        for t in range(steps)
    ]
    return gathered, residual


def moe_finish(gathered, meta, residual, topk, w_gate, w_up, w_down):
    steps, rows, model_width = residual.shape
    n_dp = lax.axis_size("dp")
    n_ex = lax.axis_size("expert")
    local_experts = w_gate.shape[0]
    all_rows = gathered[..., :model_width]
    all_gates = meta[..., :topk]
    all_ids = jnp.round(meta[..., topk : 2 * topk]).astype(jnp.int32)
    first = lax.axis_index("expert") * local_experts
    numbers = first + jnp.arange(local_experts, dtype=jnp.int32)
    matches = all_ids[..., None] == numbers
    picked = jnp.any(matches, axis=-2).astype(jnp.int32)
    gate_of = jnp.sum(jnp.where(matches, all_gates[..., None].astype(jnp.float32), 0.0), axis=-2)
    earlier = jnp.cumsum(picked, axis=2) - picked
    ranks = jnp.arange(MOST, dtype=jnp.int32)
    sender = (picked[..., None] > 0) & (earlier[..., None] == ranks)
    slots = jnp.einsum(
        "tbrxm,tbrd->tbxmd",
        sender.astype(jnp.bfloat16),
        all_rows,
        preferred_element_type=jnp.float32,
    ).astype(jnp.bfloat16)
    gate_part = jnp.einsum("tbxmd,xdf->tbxmf", slots, w_gate, preferred_element_type=jnp.float32)
    up_part = jnp.einsum("tbxmd,xdf->tbxmf", slots, w_up, preferred_element_type=jnp.float32)
    hidden_act = ((up_part + 1.0) * gate_part * jax.nn.sigmoid(1.702 * gate_part)).astype(
        jnp.bfloat16
    )
    partial = jnp.einsum(
        "tbxmf,xfd->tbxmd", hidden_act, w_down, preferred_element_type=jnp.float32
    ).astype(jnp.bfloat16)
    weights = jnp.where(sender, gate_of[..., None], 0.0).astype(jnp.bfloat16)
    grid = (steps, n_dp, n_ex)
    if local_experts * MOST < rows:
        summed = lax.psum_scatter(
            partial.astype(jnp.float32).reshape(grid + partial.shape[2:]),
            "dp",
            scatter_dimension=1,
            tiled=True,
        )[:, 0]
        own = lax.axis_index("dp")
        own_weights = lax.dynamic_index_in_dim(weights.reshape(grid + weights.shape[2:]), own, 1, False)
        row_terms = jnp.einsum(
            "terxm,texmd->terd",
            own_weights.astype(jnp.float32),
            summed,
            precision=lax.Precision.HIGHEST,
            preferred_element_type=jnp.float32,
        )
    else:
        row_terms = jnp.einsum(
            "tbrxm,tbxmd->btrd", weights, partial, preferred_element_type=jnp.float32
        ).astype(jnp.bfloat16)
        row_terms = lax.psum_scatter(
            row_terms.reshape((n_dp, n_ex) + row_terms.shape[1:]), "dp", scatter_dimension=0, tiled=True
        )[0]
        row_terms = jnp.moveaxis(row_terms, 0, 1)
    branch_out = lax.psum_scatter(row_terms, "expert", scatter_dimension=1, tiled=True)
    return (residual + branch_out[:, 0].astype(jnp.float32)).astype(jnp.bfloat16)


def body(
    hidden,
    norm_gain,
    router,
    routes,
    w_gate,
    w_up,
    w_down,
    queries,
    new_key,
    new_value,
    key_pages,
    value_pages,
    page_counts,
    page_order,
):
    host_keys, host_values = (
        lax.all_to_all(key_pages, "dp", split_axis=0, concat_axis=0, tiled=True),
        lax.all_to_all(value_pages, "dp", split_axis=0, concat_axis=0, tiled=True),
    )
    kv_width = KV_HEADS * HEAD_DIM
    space_keys = host_keys.reshape(-1, BLOCK, kv_width)
    space_values = host_values.reshape(-1, BLOCK, kv_width)
    gathered, residual = moe_layer(hidden, norm_gain, router, routes, w_gate, w_up, w_down)
    context = attention(
        queries, new_key, new_value, space_keys, space_values, page_counts[0], page_order[0]
    )
    metas = [g[..., hidden.shape[-1] :] for g in gathered]
    first, first_meta, context = lax.optimization_barrier((gathered[0], metas[0], context))
    gathered[0], metas[0] = first, first_meta
    layer_out = jnp.concatenate(
        [
            moe_finish(g, m, residual[t : t + 1], routes.shape[-1], w_gate, w_up, w_down)
            for t, (g, m) in enumerate(zip(gathered, metas))
        ],
        axis=0,
    )
    return (context, layer_out)


def solution(mesh):
    return jax.shard_map(
        body,
        mesh=mesh,
        in_specs=(
            P(None, ("dp", "expert"), None),
            P(),
            P(),
            P(None, ("dp", "expert"), None),
            P("expert", None, "dp"),
            P("expert", None, "dp"),
            P("expert", "dp", None),
            P(None, ("dp", "expert"), None),
            P(None, ("dp", "expert"), None),
            P(None, ("dp", "expert"), None),
            P(("dp", "expert"), None, None, None),
            P(("dp", "expert"), None, None, None),
            P(("dp", "expert"), None),
            P(("dp", "expert"), None),
        ),
        out_specs=(P(None, ("dp", "expert"), None), P(None, ("dp", "expert"), None)),
        check_vma=False,
    )
```

```python
import jax
import jax.numpy as jnp
from jax import lax
from jax.sharding import PartitionSpec as P

HEADS = 64
KV_HEADS = 8
HEAD_DIM = 64
EXPERTS = 64
MOST = 2
STEPS = 2
BLOCK = 16


def page_layout(counts, page_perm, most_pages):
    starts = jnp.cumsum(counts) - counts
    offsets = jnp.arange(most_pages, dtype=jnp.int32)
    places = starts[:, None] + offsets[None, :]
    places = jnp.where(offsets[None, :] < counts[:, None], places, 0)
    return jnp.take(page_perm, places, axis=0)


def attention(query_rows, fresh_keys, fresh_values, space_keys, space_values, counts, page_perm):
    group_size = HEADS // KV_HEADS
    most_pages = page_perm.shape[0] // 3
    row_count = counts.shape[0]
    cache_span = most_pages * BLOCK
    slot_ids = page_layout(counts, page_perm, most_pages).reshape(-1)
    cache_keys = jnp.take(space_keys, slot_ids, axis=0).reshape(
        row_count, cache_span, KV_HEADS, HEAD_DIM
    )
    cache_values = jnp.take(space_values, slot_ids, axis=0).reshape(
        row_count, cache_span, KV_HEADS, HEAD_DIM
    )
    live_mask = jnp.arange(cache_span)[None, :] < (counts * BLOCK)[:, None]
    query_heads = query_rows.reshape(STEPS, row_count, KV_HEADS, group_size, HEAD_DIM)
    new_keys = fresh_keys.reshape(STEPS, row_count, KV_HEADS, HEAD_DIM)
    new_values = fresh_values.reshape(STEPS, row_count, KV_HEADS, HEAD_DIM)
    score_scale = HEAD_DIM ** (-0.5)
    old_scores = (
        jnp.einsum("trkgh,rlkh->trkgl", query_heads, cache_keys, preferred_element_type=jnp.float32)
        * score_scale
    )
    old_scores = jnp.where(live_mask[None, :, None, None, :], old_scores, -jnp.inf)
    new_scores = (
        jnp.einsum("trkgh,urkh->trkgu", query_heads, new_keys, preferred_element_type=jnp.float32)
        * score_scale
    )
    causal = jnp.arange(STEPS)[None, :] <= jnp.arange(STEPS)[:, None]
    new_scores = jnp.where(causal[:, None, None, None, :], new_scores, -jnp.inf)
    row_max = jnp.maximum(jnp.max(old_scores, axis=-1), jnp.max(new_scores, axis=-1))
    old_probs = jnp.exp(old_scores - row_max[..., None])
    new_probs = jnp.exp(new_scores - row_max[..., None])
    denominator = jnp.sum(old_probs, axis=-1) + jnp.sum(new_probs, axis=-1)
    numerator = jnp.einsum(
        "trkgl,rlkh->trkgh",
        old_probs.astype(jnp.bfloat16),
        cache_values,
        preferred_element_type=jnp.float32,
    )
    numerator = numerator + jnp.einsum(
        "trkgu,urkh->trkgh",
        new_probs.astype(jnp.bfloat16),
        new_values,
        preferred_element_type=jnp.float32,
    )
    result = numerator / denominator[..., None]
    return result.reshape(STEPS, row_count, HEADS * HEAD_DIM).astype(jnp.bfloat16)


MOST = 2


def moe_layer(hidden, norm_gain, router, routes, w_gate, w_up, w_down):
    steps, rows, model_width = hidden.shape
    topk = routes.shape[-1]
    n_dp = lax.axis_size("dp")
    n_ex = lax.axis_size("expert")
    local_experts = w_gate.shape[0]
    blocks = n_dp * n_ex
    residual = hidden.astype(jnp.float32)
    scale_rows = lax.rsqrt(jnp.mean(residual * residual, axis=-1, keepdims=True) + 1e-05)
    normed = (residual * scale_rows * norm_gain).astype(jnp.bfloat16)
    logit_rows = jnp.einsum("trd,de->tre", normed, router, preferred_element_type=jnp.float32)
    chosen = jnp.take_along_axis(logit_rows, routes, axis=-1)
    spreads = chosen[..., None, :] - chosen[..., :, None]
    gate_vals = (1.0 / jnp.sum(jnp.exp(spreads), axis=-1)).astype(jnp.bfloat16)
    lanes = -(-(model_width + 2 * topk) // 128) * 128
    filler = jnp.zeros((steps, rows, lanes - model_width - 2 * topk), jnp.bfloat16)
    payload = jnp.concatenate(
        [normed, gate_vals, routes.astype(jnp.bfloat16), filler], axis=-1
    )
    gathered = lax.all_gather(payload, ("dp", "expert"), axis=1, tiled=False)
    return gathered, residual


def moe_finish(gathered, meta, residual, topk, w_gate, w_up, w_down):
    steps, rows, model_width = residual.shape
    n_dp = lax.axis_size("dp")
    n_ex = lax.axis_size("expert")
    local_experts = w_gate.shape[0]
    all_rows = gathered[..., :model_width]
    all_gates = meta[..., :topk]
    all_ids = jnp.round(meta[..., topk : 2 * topk]).astype(jnp.int32)
    first = lax.axis_index("expert") * local_experts
    numbers = first + jnp.arange(local_experts, dtype=jnp.int32)
    matches = all_ids[..., None] == numbers
    picked = jnp.any(matches, axis=-2).astype(jnp.int32)
    gate_of = jnp.sum(jnp.where(matches, all_gates[..., None].astype(jnp.float32), 0.0), axis=-2)
    earlier = jnp.cumsum(picked, axis=2) - picked
    ranks = jnp.arange(MOST, dtype=jnp.int32)
    sender = (picked[..., None] > 0) & (earlier[..., None] == ranks)
    slots = jnp.einsum(
        "tbrxm,tbrd->tbxmd",
        sender.astype(jnp.bfloat16),
        all_rows,
        preferred_element_type=jnp.float32,
    ).astype(jnp.bfloat16)
    gate_part = jnp.einsum("tbxmd,xdf->tbxmf", slots, w_gate, preferred_element_type=jnp.float32)
    up_part = jnp.einsum("tbxmd,xdf->tbxmf", slots, w_up, preferred_element_type=jnp.float32)
    hidden_act = ((up_part + 1.0) * gate_part * jax.nn.sigmoid(1.702 * gate_part)).astype(
        jnp.bfloat16
    )
    partial = jnp.einsum(
        "tbxmf,xfd->tbxmd", hidden_act, w_down, preferred_element_type=jnp.float32
    ).astype(jnp.bfloat16)
    weights = jnp.where(sender, gate_of[..., None], 0.0).astype(jnp.bfloat16)
    grid = (steps, n_dp, n_ex)
    if local_experts * MOST < rows:
        summed = lax.psum_scatter(
            partial.astype(jnp.float32).reshape(grid + partial.shape[2:]),
            "dp",
            scatter_dimension=1,
            tiled=True,
        )[:, 0]
        own = lax.axis_index("dp")
        own_weights = lax.dynamic_index_in_dim(weights.reshape(grid + weights.shape[2:]), own, 1, False)
        row_terms = jnp.einsum(
            "terxm,texmd->terd",
            own_weights.astype(jnp.float32),
            summed,
            precision=lax.Precision.HIGHEST,
            preferred_element_type=jnp.float32,
        )
    else:
        row_terms = jnp.einsum(
            "tbrxm,tbxmd->btrd", weights, partial, preferred_element_type=jnp.float32
        ).astype(jnp.bfloat16)
        row_terms = lax.psum_scatter(
            row_terms.reshape((n_dp, n_ex) + row_terms.shape[1:]), "dp", scatter_dimension=0, tiled=True
        )[0]
        shares = lax.all_to_all(row_terms, "expert", split_axis=0, concat_axis=0, tiled=True)
        branch_out = jnp.sum(shares.astype(jnp.float32), axis=0)
        return (residual + branch_out).astype(jnp.bfloat16)
    branch_out = lax.psum_scatter(row_terms, "expert", scatter_dimension=1, tiled=True)
    return (residual + branch_out[:, 0].astype(jnp.float32)).astype(jnp.bfloat16)


def body(
    hidden,
    norm_gain,
    router,
    routes,
    w_gate,
    w_up,
    w_down,
    queries,
    new_key,
    new_value,
    key_pages,
    value_pages,
    page_counts,
    page_order,
):
    host_keys, host_values = (
        lax.all_to_all(key_pages, "dp", split_axis=0, concat_axis=0, tiled=True),
        lax.all_to_all(value_pages, "dp", split_axis=0, concat_axis=0, tiled=True),
    )
    kv_width = KV_HEADS * HEAD_DIM
    space_keys = host_keys.reshape(-1, BLOCK, kv_width)
    space_values = host_values.reshape(-1, BLOCK, kv_width)
    gathered, residual = moe_layer(hidden, norm_gain, router, routes, w_gate, w_up, w_down)
    context = attention(
        queries, new_key, new_value, space_keys, space_values, page_counts[0], page_order[0]
    )
    meta = gathered[..., hidden.shape[-1] :]
    gathered, meta, context = lax.optimization_barrier((gathered, meta, context))
    layer_out = moe_finish(gathered, meta, residual, routes.shape[-1], w_gate, w_up, w_down)
    return (context, layer_out)


def solution(mesh):
    return jax.shard_map(
        body,
        mesh=mesh,
        in_specs=(
            P(None, ("dp", "expert"), None),
            P(),
            P(),
            P(None, ("dp", "expert"), None),
            P("expert", None, "dp"),
            P("expert", None, "dp"),
            P("expert", "dp", None),
            P(None, ("dp", "expert"), None),
            P(None, ("dp", "expert"), None),
            P(None, ("dp", "expert"), None),
            P(("dp", "expert"), None, None, None),
            P(("dp", "expert"), None, None, None),
            P(("dp", "expert"), None),
            P(("dp", "expert"), None),
        ),
        out_specs=(P(None, ("dp", "expert"), None), P(None, ("dp", "expert"), None)),
        check_vma=False,
    )
```

```python
import jax
import jax.numpy as jnp
from jax import lax
from jax.sharding import PartitionSpec as P

HEADS = 64
KV_HEADS = 8
HEAD_DIM = 64
EXPERTS = 64
MOST = 2
STEPS = 2
BLOCK = 16


def page_layout(counts, page_perm, most_pages):
    starts = jnp.cumsum(counts) - counts
    offsets = jnp.arange(most_pages, dtype=jnp.int32)
    places = starts[:, None] + offsets[None, :]
    places = jnp.where(offsets[None, :] < counts[:, None], places, 0)
    return jnp.take(page_perm, places, axis=0)


def attention(query_rows, fresh_keys, fresh_values, space_keys, space_values, counts, page_perm):
    group_size = HEADS // KV_HEADS
    most_pages = page_perm.shape[0] // 3
    row_count = counts.shape[0]
    cache_span = most_pages * BLOCK
    slot_ids = page_layout(counts, page_perm, most_pages).reshape(-1)
    cache_keys = jnp.take(space_keys, slot_ids, axis=0).reshape(
        row_count, cache_span, KV_HEADS, HEAD_DIM
    )
    cache_values = jnp.take(space_values, slot_ids, axis=0).reshape(
        row_count, cache_span, KV_HEADS, HEAD_DIM
    )
    live_mask = jnp.arange(cache_span)[None, :] < (counts * BLOCK)[:, None]
    query_heads = query_rows.reshape(STEPS, row_count, KV_HEADS, group_size, HEAD_DIM)
    new_keys = fresh_keys.reshape(STEPS, row_count, KV_HEADS, HEAD_DIM)
    new_values = fresh_values.reshape(STEPS, row_count, KV_HEADS, HEAD_DIM)
    score_scale = HEAD_DIM ** (-0.5)
    old_scores = (
        jnp.einsum("trkgh,rlkh->trkgl", query_heads, cache_keys, preferred_element_type=jnp.float32)
        * score_scale
    )
    old_scores = jnp.where(live_mask[None, :, None, None, :], old_scores, -jnp.inf)
    new_scores = (
        jnp.einsum("trkgh,urkh->trkgu", query_heads, new_keys, preferred_element_type=jnp.float32)
        * score_scale
    )
    causal = jnp.arange(STEPS)[None, :] <= jnp.arange(STEPS)[:, None]
    new_scores = jnp.where(causal[:, None, None, None, :], new_scores, -jnp.inf)
    row_max = jnp.maximum(jnp.max(old_scores, axis=-1), jnp.max(new_scores, axis=-1))
    old_probs = jnp.exp(old_scores - row_max[..., None])
    new_probs = jnp.exp(new_scores - row_max[..., None])
    denominator = jnp.sum(old_probs, axis=-1) + jnp.sum(new_probs, axis=-1)
    numerator = jnp.einsum(
        "trkgl,rlkh->trkgh",
        old_probs.astype(jnp.bfloat16),
        cache_values,
        preferred_element_type=jnp.float32,
    )
    numerator = numerator + jnp.einsum(
        "trkgu,urkh->trkgh",
        new_probs.astype(jnp.bfloat16),
        new_values,
        preferred_element_type=jnp.float32,
    )
    result = numerator / denominator[..., None]
    return result.reshape(STEPS, row_count, HEADS * HEAD_DIM).astype(jnp.bfloat16)


MOST = 2


def moe_layer(hidden, norm_gain, router, routes, w_gate, w_up, w_down):
    steps, rows, model_width = hidden.shape
    topk = routes.shape[-1]
    n_dp = lax.axis_size("dp")
    n_ex = lax.axis_size("expert")
    local_experts = w_gate.shape[0]
    blocks = n_dp * n_ex
    residual = hidden.astype(jnp.float32)
    scale_rows = lax.rsqrt(jnp.mean(residual * residual, axis=-1, keepdims=True) + 1e-05)
    normed = (residual * scale_rows * norm_gain).astype(jnp.bfloat16)
    logit_rows = jnp.einsum("trd,de->tre", normed, router, preferred_element_type=jnp.float32)
    chosen = jnp.take_along_axis(logit_rows, routes, axis=-1)
    spreads = chosen[..., None, :] - chosen[..., :, None]
    gate_vals = (1.0 / jnp.sum(jnp.exp(spreads), axis=-1)).astype(jnp.bfloat16)
    lanes = -(-(model_width + 2 * topk) // 128) * 128
    filler = jnp.zeros((steps, rows, lanes - model_width - 2 * topk), jnp.bfloat16)
    payload = jnp.concatenate(
        [normed, gate_vals, routes.astype(jnp.bfloat16), filler], axis=-1
    )
    gathered = lax.all_gather(payload, ("dp", "expert"), axis=1, tiled=False)
    return gathered, residual


def moe_finish(gathered, meta, residual, topk, w_gate, w_up, w_down):
    steps, rows, model_width = residual.shape
    n_dp = lax.axis_size("dp")
    n_ex = lax.axis_size("expert")
    local_experts = w_gate.shape[0]
    all_rows = gathered[..., :model_width]
    all_gates = meta[..., :topk]
    all_ids = jnp.round(meta[..., topk : 2 * topk]).astype(jnp.int32)
    first = lax.axis_index("expert") * local_experts
    numbers = first + jnp.arange(local_experts, dtype=jnp.int32)
    matches = all_ids[..., None] == numbers
    picked = jnp.any(matches, axis=-2).astype(jnp.int32)
    gate_of = jnp.sum(jnp.where(matches, all_gates[..., None].astype(jnp.float32), 0.0), axis=-2)
    earlier = jnp.cumsum(picked, axis=2) - picked
    ranks = jnp.arange(MOST, dtype=jnp.int32)
    sender = (picked[..., None] > 0) & (earlier[..., None] == ranks)
    slots = jnp.einsum(
        "tbrxm,tbrd->tbxmd",
        sender.astype(jnp.bfloat16),
        all_rows,
        preferred_element_type=jnp.float32,
    ).astype(jnp.bfloat16)
    gate_part = jnp.einsum("tbxmd,xdf->tbxmf", slots, w_gate, preferred_element_type=jnp.float32)
    up_part = jnp.einsum("tbxmd,xdf->tbxmf", slots, w_up, preferred_element_type=jnp.float32)
    hidden_act = ((up_part + 1.0) * gate_part * jax.nn.sigmoid(1.702 * gate_part)).astype(
        jnp.bfloat16
    )
    partial = jnp.einsum(
        "tbxmf,xfd->tbxmd", hidden_act, w_down, preferred_element_type=jnp.float32
    ).astype(jnp.bfloat16)
    weights = jnp.where(sender, gate_of[..., None], 0.0).astype(jnp.bfloat16)
    grid = (steps, n_dp, n_ex)
    if local_experts * MOST < rows:
        summed = lax.psum_scatter(
            partial.astype(jnp.float32).reshape(grid + partial.shape[2:]),
            "dp",
            scatter_dimension=1,
            tiled=True,
        )[:, 0]
        own = lax.axis_index("dp")
        own_weights = lax.dynamic_index_in_dim(weights.reshape(grid + weights.shape[2:]), own, 1, False)
        row_terms = jnp.einsum(
            "terxm,texmd->terd",
            own_weights.astype(jnp.float32),
            summed,
            precision=lax.Precision.HIGHEST,
            preferred_element_type=jnp.float32,
        )
    else:
        row_terms = jnp.einsum(
            "tbrxm,tbxmd->btrd", weights, partial, preferred_element_type=jnp.float32
        ).astype(jnp.bfloat16)
        row_terms = lax.all_to_all(
            row_terms.reshape((n_dp, n_ex) + row_terms.shape[1:]), "dp", split_axis=0, concat_axis=0, tiled=True
        )
        row_terms = jnp.sum(row_terms.astype(jnp.float32), axis=0).astype(jnp.bfloat16)
        shares = lax.all_to_all(row_terms, "expert", split_axis=0, concat_axis=0, tiled=True)
        branch_out = jnp.sum(shares.astype(jnp.float32), axis=0)
        return (residual + branch_out).astype(jnp.bfloat16)
    branch_out = lax.psum_scatter(row_terms, "expert", scatter_dimension=1, tiled=True)
    return (residual + branch_out[:, 0].astype(jnp.float32)).astype(jnp.bfloat16)


def body(
    hidden,
    norm_gain,
    router,
    routes,
    w_gate,
    w_up,
    w_down,
    queries,
    new_key,
    new_value,
    key_pages,
    value_pages,
    page_counts,
    page_order,
):
    host_keys, host_values = (
        lax.all_to_all(key_pages, "dp", split_axis=0, concat_axis=0, tiled=True),
        lax.all_to_all(value_pages, "dp", split_axis=0, concat_axis=0, tiled=True),
    )
    kv_width = KV_HEADS * HEAD_DIM
    space_keys = host_keys.reshape(-1, BLOCK, kv_width)
    space_values = host_values.reshape(-1, BLOCK, kv_width)
    gathered, residual = moe_layer(hidden, norm_gain, router, routes, w_gate, w_up, w_down)
    context = attention(
        queries, new_key, new_value, space_keys, space_values, page_counts[0], page_order[0]
    )
    meta = gathered[..., hidden.shape[-1] :]
    gathered, meta, context = lax.optimization_barrier((gathered, meta, context))
    layer_out = moe_finish(gathered, meta, residual, routes.shape[-1], w_gate, w_up, w_down)
    return (context, layer_out)


def solution(mesh):
    return jax.shard_map(
        body,
        mesh=mesh,
        in_specs=(
            P(None, ("dp", "expert"), None),
            P(),
            P(),
            P(None, ("dp", "expert"), None),
            P("expert", None, "dp"),
            P("expert", None, "dp"),
            P("expert", "dp", None),
            P(None, ("dp", "expert"), None),
            P(None, ("dp", "expert"), None),
            P(None, ("dp", "expert"), None),
            P(("dp", "expert"), None, None, None),
            P(("dp", "expert"), None, None, None),
            P(("dp", "expert"), None),
            P(("dp", "expert"), None),
        ),
        out_specs=(P(None, ("dp", "expert"), None), P(None, ("dp", "expert"), None)),
        check_vma=False,
    )
```
